256 devices in a mesh: tm: 64 (over z, x_hi, y), chan: 4 (over x_lo, core).
Axes of the slice: x: 4 (x_hi: 2, x_lo: 2; x = x_hi * 2 + x_lo), y: 4, z: 8, core: 2. Of those that a mesh axis runs over, the one named last changes fastest.
Arguments:
- signal: float32 [256, 8192], P('chan', 'tm'), may hold values from -256 to 256
- support: int32 [32], replicated, may hold values from 1 to 4, as said below
- pair_first: int32 [4, 512], replicated, may hold values from 0 to 255
- pair_second: int32 [4, 512], replicated, may hold values from 0 to 255
- pair_count: int32 [4], replicated, may hold values from 128 to 512, as said below
Outputs:
- cross: float32 [4, 512, 2, 32], P('chan', 'tm')
- coherence: float32 [4, 512, 32], P('chan', 'tm')
The draws below stay inside these ranges and needn't reach their ends.
Inputs may be any that keep to these rules, and one draw needn't show every extreme that they name: With b = q // 8 the band of scale q, support[q] is at most (4 * 128 / 4^(3 - b) + 127) // 128, and equals it for the last scale of every band. The live slots of an owner are its first pair_count slots; some owner has all 512 slots live.
All inputs are finite; a program needn't handle non-finite values.
Results may differ from the reference program's by a relative error of at most 0.0027.
Values may be sent and summed in bfloat16 or wider, within the bound.
No kernel may reach another device: no remote copies, remote signals or barrier semaphores. Data moves between devices by JAX's collectives and lax.ppermute only.
A program may use at most 192 MiB of HBM per device.

```python
import math
import jax
import jax.numpy as jnp
from jax import lax

CH = 256
NS = 32
BLK = 128
TD = 128
NT = 8192
OWNERS = 4
CAP = 512


def draw_signal(key, part):
    subkeys = jax.random.split(key, 6)
    common = jnp.clip(jax.random.normal(subkeys[0], (8, NT), jnp.float32), -6.0, 6.0)
    source = jax.random.randint(subkeys[1], (CH,), 0, 8)
    delays = jax.random.randint(subkeys[2], (CH,), 0, 2 * TD)
    direct = jax.random.uniform(subkeys[3], (CH, 1), jnp.float32, 0.5, 1.5)
    echoes = jax.random.uniform(subkeys[4], (CH, 1), jnp.float32, -1.0, 1.0)
    sample_index = jnp.arange(NT, dtype=jnp.int32)
    lagged_signal = (sample_index[None, :] - delays[:, None]) % NT
    mixture = direct * common[source] + echoes * common[source[:, None], lagged_signal]
    averaged = 0.25 * (mixture + jnp.roll(mixture, 1, axis=1) + jnp.roll(mixture, 2, axis=1) + jnp.roll(mixture, 3, axis=1))
    averaged_frequency_content = jnp.clip(1.6 * averaged, -6.5, 6.5)
    odd_even_marker = (1 - 2 * (sample_index % 2)).astype(jnp.float32)
    oscillating_factor = 1.0 + 2.0 * odd_even_marker
    bell_decay_factor = jnp.exp(0.5 * math.log(3.0) * sample_index.astype(jnp.float32) / NT)
    local_portion = 0.3 * jnp.clip(jax.random.normal(subkeys[5], (CH, NT), jnp.float32), -4.0, 4.0)
    sensor_lead_multiplier = jnp.ones((CH, 1), jnp.float32)
    return (sensor_lead_multiplier * bell_decay_factor[None, :] * (averaged_frequency_content * oscillating_factor[None, :] + local_portion)).astype(jnp.float32)


def draw_support(key, part):
    first_key, second_key = jax.random.split(key)
    scale_index = jnp.arange(NS, dtype=jnp.int32)
    band_index = scale_index // (NS // 4)
    widest = (4 * TD // jnp.power(4, 3 - band_index) + BLK - 1) // BLK
    first_reach = jax.random.randint(first_key, (NS,), 1, widest + 1)
    second_reach = jax.random.randint(second_key, (NS,), 1, widest + 1)
    drawn_reach = jnp.minimum(first_reach, second_reach)
    return jnp.where(scale_index % (NS // 4) == NS // 4 - 1, widest, drawn_reach).astype(jnp.int32)


def draw_pair_count(key, part):
    first_key, second_key = jax.random.split(key)
    counts = jax.random.randint(first_key, (OWNERS,), CAP // 4, CAP + 1)
    full_owner = jax.random.randint(second_key, (), 0, OWNERS)
    return jnp.where(jnp.arange(OWNERS) == full_owner, CAP, counts).astype(jnp.int32)


def place_ends(values, own_key, least, largest):
    place = [jax.random.randint(jax.random.fold_in(own_key, axis), (), 0, length) for axis, length in enumerate(values.shape)]
    widest = values.shape.index(max(values.shape))
    next_to = place[:widest] + [(place[widest] + 1) % values.shape[widest]] + place[widest + 1:]
    return values.at[tuple(place)].set(least).at[tuple(next_to)].set(largest)


def setup_inputs(seed: int = 0) -> dict:
    splits = jax.random.split(jax.random.key(seed), 6)
    return {
        "signal": draw_signal(jax.random.fold_in(splits[5], 71), 0),
        "support": draw_support(jax.random.fold_in(splits[5], 71), 0),
        "pair_first": place_ends(jax.random.randint(splits[2], (OWNERS, CAP), 0, CH), jax.random.fold_in(splits[2], 1), 0, CH - 1).astype(jnp.int32),
        "pair_second": place_ends(jax.random.randint(splits[3], (OWNERS, CAP), 0, CH), jax.random.fold_in(splits[3], 1), 0, CH - 1).astype(jnp.int32),
        "pair_count": draw_pair_count(jax.random.fold_in(splits[5], 71), 0),
    }


def morlet_parts(offset, scale_index, reach_blocks):
    scale_width = 2.0 * TD * jnp.exp2((scale_index - (NS - 1)).astype(jnp.float32) / 4.0)
    scaled_offset = offset.astype(jnp.float32) / scale_width
    amplitude = math.pi ** (-0.25) * lax.rsqrt(scale_width) * jnp.exp(-0.5 * scaled_offset * scaled_offset)
    inside = jnp.abs(offset) < reach_blocks * BLK
    real_part = jnp.where(inside, amplitude * jnp.cos(6.0 * scaled_offset), 0.0)
    imag_part = jnp.where(inside, amplitude * jnp.sin(6.0 * scaled_offset), 0.0)
    return (real_part.astype(jnp.bfloat16), imag_part.astype(jnp.bfloat16))

def reference(signal, support, pair_first, pair_second, pair_count):
    ntime = signal.shape[1]
    rounded = lax.optimization_barrier(signal.astype(jnp.bfloat16)).astype(jnp.float32)
    spectrum = jnp.fft.fft(rounded, axis=1)
    position = jnp.arange(ntime, dtype=jnp.int32)
    signed = jnp.where(position <= ntime // 2, position, position - ntime)
    slot_index = jnp.arange(CAP, dtype=jnp.int32)
    alive_mask = slot_index[None, :] < pair_count[:, None]
    first_flat = pair_first.reshape(-1)
    second_flat = pair_second.reshape(-1)
    pair_total = first_flat.shape[0]
    block_pairs = math.gcd(pair_total, 128)
    first_blocks = first_flat.reshape(-1, block_pairs)
    second_blocks = second_flat.reshape(-1, block_pairs)

    def single_scale(scale_index):
        kernel_real, kernel_imag = morlet_parts(signed, scale_index, support[scale_index])
        kernel_real = lax.optimization_barrier(kernel_real).astype(jnp.float32)
        kernel_imag = lax.optimization_barrier(kernel_imag).astype(jnp.float32)
        response = jnp.fft.ifft(kernel_real + 1j * kernel_imag) * ntime
        coefficients = jnp.fft.ifft(spectrum * response[None, :], axis=1)
        coef_real = lax.optimization_barrier(coefficients.real.astype(jnp.bfloat16)).astype(jnp.float32)
        coef_imag = lax.optimization_barrier(coefficients.imag.astype(jnp.bfloat16)).astype(jnp.float32)
        auto_power = lax.optimization_barrier(jnp.sum(coef_real * coef_real + coef_imag * coef_imag, axis=1)) / ntime

        def pair_block(block_index):
            first_member_number = first_blocks[block_index]
            right_index = second_blocks[block_index]
            left_real = coef_real[first_member_number]
            left_imag = coef_imag[first_member_number]
            right_real = coef_real[right_index]
            right_imag = coef_imag[right_index]
            cross_real = lax.optimization_barrier(jnp.sum(left_real * right_real + left_imag * right_imag, axis=1)) / ntime
            cross_imag = lax.optimization_barrier(jnp.sum(left_imag * right_real - left_real * right_imag, axis=1)) / ntime
            return (cross_real, cross_imag)
        cross_real, cross_imag = lax.map(pair_block, jnp.arange(first_blocks.shape[0], dtype=jnp.int32))
        return (cross_real.reshape(-1), cross_imag.reshape(-1), auto_power)
    cross_real, cross_imag, auto_power = lax.map(single_scale, jnp.arange(NS, dtype=jnp.int32))
    first_power = auto_power[:, first_flat]
    second_power = auto_power[:, second_flat]
    coherence = (cross_real * cross_real + cross_imag * cross_imag) / ((first_power + 1e-06) * (second_power + 1e-06))
    owner_devices = pair_first.shape[0]
    stacked = jnp.stack([cross_real, cross_imag], axis=0).reshape(2, NS, owner_devices, CAP).transpose(2, 3, 0, 1)
    cross = jnp.where(alive_mask[:, :, None, None], stacked, 0.0)
    coherence = coherence.reshape(NS, owner_devices, CAP).transpose(1, 2, 0)
    coherence = jnp.where(alive_mask[:, :, None], coherence, 0.0)
    return (cross, coherence)
```

```python
import math

import jax
import jax.numpy as jnp
import numpy as np
from jax import lax
from jax.sharding import PartitionSpec as P

NS = 32
BLK = 128
TD = 128


power_floor = 1e-06


def from_behind(array, axis, by):
    peers = lax.axis_size(axis)
    return lax.ppermute(array, axis, [(i, (i + by) % peers) for i in range(peers)])


def morlet_parts(offset, scale_index, reach_blocks):
    scale_width = 2.0 * TD * jnp.exp2((scale_index - (NS - 1)).astype(jnp.float32) / 4.0)
    scaled_offset = offset.astype(jnp.float32) / scale_width
    amplitude = (
        math.pi ** (-0.25) * lax.rsqrt(scale_width) * jnp.exp(-0.5 * scaled_offset * scaled_offset)
    )
    inside = jnp.abs(offset) < reach_blocks * BLK
    real_part = jnp.where(inside, amplitude * jnp.cos(6.0 * scaled_offset), 0.0)
    imag_part = jnp.where(inside, amplitude * jnp.sin(6.0 * scaled_offset), 0.0)
    return (real_part.astype(jnp.bfloat16), imag_part.astype(jnp.bfloat16))


def wavelet_band(extended, scale_ids, reaches, offsets, time_span):
    channels = extended.shape[0]
    blocks = time_span // BLK
    centre = 4 * time_span // BLK
    tap_blocks = 2 * offsets + 1
    pieces = [
        extended[:, (centre + offset_step) * BLK : (centre + offset_step) * BLK + time_span]
        for offset_step in range(-offsets, offsets + 1)
    ]
    unfolded = jnp.stack(pieces, axis=1).reshape(channels, tap_blocks, blocks, BLK)
    unfolded = unfolded.transpose(0, 2, 1, 3).reshape(channels * blocks, tap_blocks * BLK)
    lag_start = (jnp.arange(tap_blocks, dtype=jnp.int32) - offsets) * BLK
    within = jnp.arange(BLK, dtype=jnp.int32)
    tap_offset = lag_start[:, None, None] + within[None, :, None] - within[None, None, :]

    def single_scale(scale_index, reach_blocks):
        return morlet_parts(tap_offset, scale_index, reach_blocks)

    real_part, imag_part = jax.vmap(single_scale)(scale_ids, reaches)
    kernel_table = jnp.stack([real_part, imag_part], axis=1)
    kernel_table = kernel_table.transpose(2, 3, 0, 1, 4).reshape(tap_blocks * BLK, -1)
    coefficients = jnp.dot(unfolded, kernel_table, preferred_element_type=jnp.float32)
    scale_count = scale_ids.shape[0]
    coefficients = coefficients.astype(jnp.bfloat16).reshape(channels, blocks, scale_count, 2, BLK)
    return coefficients.transpose(2, 3, 0, 1, 4).reshape(scale_count, 2 * channels, time_span)


def pair_sums(coefficients, first_flat, second_flat):
    scale_count = coefficients.shape[0]
    channels = coefficients.shape[1] // 2
    time_span = coefficients.shape[2]
    chan_iota = jnp.arange(channels, dtype=jnp.int32)
    both = jnp.concatenate([first_flat, second_flat])
    pick = (both[:, None] == chan_iota[None, :]).astype(jnp.bfloat16)
    parts = coefficients.reshape(scale_count, 2, channels, time_span)
    picked = jnp.einsum("pc,qrct->qrpt", pick, parts, preferred_element_type=jnp.float32)
    picked = picked.astype(jnp.bfloat16).astype(jnp.float32)
    pairs = first_flat.shape[0]
    first_real = picked[:, 0, :pairs]
    first_imag = picked[:, 1, :pairs]
    second_real = picked[:, 0, pairs:]
    second_imag = picked[:, 1, pairs:]
    cross_real = jnp.sum(first_real * second_real + first_imag * second_imag, axis=-1)
    cross_imag = jnp.sum(first_imag * second_real - first_real * second_imag, axis=-1)
    power_first = jnp.sum(first_real * first_real + first_imag * first_imag, axis=-1)
    power_second = jnp.sum(second_real * second_real + second_imag * second_imag, axis=-1)
    return jnp.stack([cross_real, cross_imag, power_first, power_second], axis=1)


def shards(signal, support, pair_first, pair_second, pair_count):
    groups = lax.axis_size("chan")
    cluster_number = lax.axis_index("chan")
    time_index = lax.axis_index("tm")
    time_devices = lax.axis_size("tm")
    time_span = signal.shape[1]
    ntime = time_span * time_devices
    rounded = signal.astype(jnp.bfloat16)
    gathered = lax.all_gather(rounded, "chan", axis=0, tiled=True)
    neighbours = [
        from_behind(gathered, "tm", distance) for distance in (4, 3, 2, 1, -1, -2, -3, -4)
    ]
    extended = jnp.concatenate(neighbours[:4] + [gathered] + neighbours[4:], axis=1)
    per_group = NS // groups
    scale_ids = cluster_number * per_group + jnp.arange(per_group, dtype=jnp.int32)
    coefficients = wavelet_band(
        extended, scale_ids, support[scale_ids], 4 * time_span // BLK, time_span
    )
    owner_devices, slots_total = pair_first.shape
    sums = pair_sums(coefficients, pair_first.reshape(-1), pair_second.reshape(-1))
    slots_local = slots_total // time_devices
    values = sums.shape[1]
    partial_value = sums.reshape(per_group, values, owner_devices, time_devices, slots_local)
    partial_value = partial_value.transpose(3, 2, 4, 1, 0)
    exchanged = lax.all_to_all(partial_value, "tm", 0, 0, tiled=True)
    summed = jnp.sum(exchanged, axis=0)
    owned = lax.all_to_all(summed, "chan", 0, 3, tiled=True)[0] / ntime
    slot_index = time_index * slots_local + jnp.arange(slots_local, dtype=jnp.int32)
    alive_mask = slot_index < pair_count[cluster_number]
    cross_real = owned[:, 0, :]
    cross_imag = owned[:, 1, :]
    first_power = owned[:, 2, :]
    second_power = owned[:, 3, :]
    coherence = (cross_real * cross_real + cross_imag * cross_imag) / (
        (first_power + power_floor) * (second_power + power_floor)
    )
    coherence = jnp.where(alive_mask[:, None], coherence, 0.0)[None]
    cross = jnp.stack([cross_real, cross_imag], axis=1)
    cross = jnp.where(alive_mask[:, None, None], cross, 0.0)[None]
    return (cross, coherence.astype(jnp.float32))


def solution(mesh):
    in_specs = (P("chan", "tm"), P(), P(), P(), P())
    out_specs = (P("chan", "tm", None, None), P("chan", "tm", None))
    return jax.shard_map(shards, mesh=mesh, in_specs=in_specs, out_specs=out_specs, check_vma=False)
```

```python
import math

import jax
import jax.numpy as jnp
import numpy as np
from jax import lax
from jax.sharding import PartitionSpec as P

NS = 32
BLK = 128
TD = 128


power_floor = 1e-06


def from_behind(array, axis, by):
    peers = lax.axis_size(axis)
    return lax.ppermute(array, axis, [(i, (i + by) % peers) for i in range(peers)])


def kernel_table(scale_ids, reaches, offsets):
    taps = (2 * offsets + 1) * BLK
    lag = jnp.arange(taps, dtype=jnp.int32) - offsets * BLK
    within = jnp.arange(BLK, dtype=jnp.int32)
    scale_width = 2.0 * TD * jnp.exp2((scale_ids - (NS - 1)).astype(jnp.float32) / 4.0)
    offset = lag[:, None, None] - within[None, None, :]
    scaled_offset = offset.astype(jnp.float32) / scale_width[None, :, None]
    amplitude = (
        math.pi ** (-0.25)
        * lax.rsqrt(scale_width)[None, :, None]
        * jnp.exp(-0.5 * scaled_offset * scaled_offset)
    )
    inside = jnp.abs(offset) < (reaches * BLK)[None, :, None]
    lag_phase = 6.0 * (lag.astype(jnp.float32)[:, None] / scale_width[None, :])
    time_phase = 6.0 * (within.astype(jnp.float32)[None, :] / scale_width[:, None])
    lag_cos = jnp.cos(lag_phase)[:, :, None]
    lag_sin = jnp.sin(lag_phase)[:, :, None]
    time_cos = jnp.cos(time_phase)[None]
    time_sin = jnp.sin(time_phase)[None]
    cos_part = lag_cos * time_cos + lag_sin * time_sin
    sin_part = lag_sin * time_cos - lag_cos * time_sin
    real_part = jnp.where(inside, amplitude * cos_part, 0.0).astype(jnp.bfloat16)
    imag_part = jnp.where(inside, amplitude * sin_part, 0.0).astype(jnp.bfloat16)
    table = jnp.stack([real_part, imag_part], axis=2)
    return table.reshape(taps, -1)


def wavelet_band(extended, scale_ids, reaches, offsets, time_span):
    channels = extended.shape[0]
    blocks = time_span // BLK
    centre = 4 * time_span // BLK
    tap_blocks = 2 * offsets + 1
    pieces = [
        extended[:, (centre + offset_step) * BLK : (centre + offset_step) * BLK + time_span]
        for offset_step in range(-offsets, offsets + 1)
    ]
    unfolded = jnp.stack(pieces, axis=1).reshape(channels, tap_blocks, blocks, BLK)
    unfolded = unfolded.transpose(0, 2, 1, 3).reshape(channels * blocks, tap_blocks * BLK)
    table = kernel_table(scale_ids, reaches, offsets)
    coefficients = jnp.dot(unfolded, table, preferred_element_type=jnp.float32)
    scale_count = scale_ids.shape[0]
    coefficients = coefficients.astype(jnp.bfloat16).reshape(channels, blocks, scale_count, 2, BLK)
    return coefficients.transpose(2, 3, 0, 1, 4).reshape(scale_count, 2 * channels, time_span)


def pair_sums(coefficients, first_flat, second_flat):
    scale_count = coefficients.shape[0]
    channels = coefficients.shape[1] // 2
    time_span = coefficients.shape[2]
    chan_iota = jnp.arange(channels, dtype=jnp.int32)
    both = jnp.concatenate([first_flat, second_flat])
    pick = (both[:, None] == chan_iota[None, :]).astype(jnp.bfloat16)
    parts = coefficients.reshape(scale_count, 2, channels, time_span)
    picked = jnp.einsum("pc,qrct->qrpt", pick, parts, preferred_element_type=jnp.float32)
    picked = picked.astype(jnp.bfloat16).astype(jnp.float32)
    pairs = first_flat.shape[0]
    first_real = picked[:, 0, :pairs]
    first_imag = picked[:, 1, :pairs]
    second_real = picked[:, 0, pairs:]
    second_imag = picked[:, 1, pairs:]
    cross_real = jnp.sum(first_real * second_real + first_imag * second_imag, axis=-1)
    cross_imag = jnp.sum(first_imag * second_real - first_real * second_imag, axis=-1)
    power_first = jnp.sum(first_real * first_real + first_imag * first_imag, axis=-1)
    power_second = jnp.sum(second_real * second_real + second_imag * second_imag, axis=-1)
    return jnp.stack([cross_real, cross_imag, power_first, power_second], axis=1)


def shards(signal, support, pair_first, pair_second, pair_count):
    groups = lax.axis_size("chan")
    cluster_number = lax.axis_index("chan")
    time_index = lax.axis_index("tm")
    time_devices = lax.axis_size("tm")
    time_span = signal.shape[1]
    ntime = time_span * time_devices
    rounded = signal.astype(jnp.bfloat16)
    gathered = lax.all_gather(rounded, "chan", axis=0, tiled=True)
    neighbours = [
        from_behind(gathered, "tm", distance) for distance in (4, 3, 2, 1, -1, -2, -3, -4)
    ]
    extended = jnp.concatenate(neighbours[:4] + [gathered] + neighbours[4:], axis=1)
    per_group = NS // groups
    scale_ids = cluster_number * per_group + jnp.arange(per_group, dtype=jnp.int32)
    coefficients = wavelet_band(
        extended, scale_ids, support[scale_ids], 4 * time_span // BLK, time_span
    )
    owner_devices, slots_total = pair_first.shape
    sums = pair_sums(coefficients, pair_first.reshape(-1), pair_second.reshape(-1))
    slots_local = slots_total // time_devices
    values = sums.shape[1]
    partial_value = sums.reshape(per_group, values, owner_devices, time_devices, slots_local)
    partial_value = partial_value.transpose(3, 2, 4, 1, 0)
    exchanged = lax.all_to_all(partial_value, "tm", 0, 0, tiled=True)
    summed = jnp.sum(exchanged, axis=0)
    owned = lax.all_to_all(summed, "chan", 0, 3, tiled=True)[0] / ntime
    slot_index = time_index * slots_local + jnp.arange(slots_local, dtype=jnp.int32)
    alive_mask = slot_index < pair_count[cluster_number]
    cross_real = owned[:, 0, :]
    cross_imag = owned[:, 1, :]
    first_power = owned[:, 2, :]
    second_power = owned[:, 3, :]
    coherence = (cross_real * cross_real + cross_imag * cross_imag) / (
        (first_power + power_floor) * (second_power + power_floor)
    )
    coherence = jnp.where(alive_mask[:, None], coherence, 0.0)[None]
    cross = jnp.stack([cross_real, cross_imag], axis=1)
    cross = jnp.where(alive_mask[:, None, None], cross, 0.0)[None]
    return (cross, coherence.astype(jnp.float32))


def solution(mesh):
    in_specs = (P("chan", "tm"), P(), P(), P(), P())
    out_specs = (P("chan", "tm", None, None), P("chan", "tm", None))
    return jax.shard_map(shards, mesh=mesh, in_specs=in_specs, out_specs=out_specs, check_vma=False)
```

```python
import math

import jax
import jax.numpy as jnp
import numpy as np
from jax import lax
from jax.sharding import PartitionSpec as P

NS = 32
BLK = 128
TD = 128


power_floor = 1e-06


def from_behind(array, axis, by):
    peers = lax.axis_size(axis)
    return lax.ppermute(array, axis, [(i, (i + by) % peers) for i in range(peers)])


def kernel_table(scale_ids, reaches, offsets):
    taps = (2 * offsets + 1) * BLK
    lag = jnp.arange(taps, dtype=jnp.int32) - offsets * BLK
    within = jnp.arange(BLK, dtype=jnp.int32)
    scale_width = 2.0 * TD * jnp.exp2((scale_ids - (NS - 1)).astype(jnp.float32) / 4.0)
    offset = lag[:, None, None] - within[None, None, :]
    scaled_offset = offset.astype(jnp.float32) / scale_width[None, :, None]
    amplitude = (
        math.pi ** (-0.25)
        * lax.rsqrt(scale_width)[None, :, None]
        * jnp.exp(-0.5 * scaled_offset * scaled_offset)
    )
    inside = jnp.abs(offset) < (reaches * BLK)[None, :, None]
    lag_phase = 6.0 * (lag.astype(jnp.float32)[:, None] / scale_width[None, :])
    time_phase = 6.0 * (within.astype(jnp.float32)[None, :] / scale_width[:, None])
    lag_cos = jnp.cos(lag_phase)[:, :, None]
    lag_sin = jnp.sin(lag_phase)[:, :, None]
    time_cos = jnp.cos(time_phase)[None]
    time_sin = jnp.sin(time_phase)[None]
    cos_part = lag_cos * time_cos + lag_sin * time_sin
    sin_part = lag_sin * time_cos - lag_cos * time_sin
    real_part = jnp.where(inside, amplitude * cos_part, 0.0).astype(jnp.bfloat16)
    imag_part = jnp.where(inside, amplitude * sin_part, 0.0).astype(jnp.bfloat16)
    table = jnp.stack([real_part, imag_part], axis=2)
    return table.reshape(taps, -1)


def wavelet_band(extended, scale_ids, reaches, offsets, time_span):
    channels = extended.shape[0]
    blocks = time_span // BLK
    centre = 4 * time_span // BLK
    tap_blocks = 2 * offsets + 1
    pieces = [
        extended[:, (centre + offset_step) * BLK : (centre + offset_step) * BLK + time_span]
        for offset_step in range(-offsets, offsets + 1)
    ]
    unfolded = jnp.stack(pieces, axis=1).reshape(channels, tap_blocks, blocks, BLK)
    unfolded = unfolded.transpose(0, 2, 1, 3).reshape(channels * blocks, tap_blocks * BLK)
    table = kernel_table(scale_ids, reaches, offsets)
    coefficients = jnp.dot(unfolded, table, preferred_element_type=jnp.float32)
    scale_count = scale_ids.shape[0]
    coefficients = coefficients.astype(jnp.bfloat16).reshape(channels, blocks, scale_count, 2, BLK)
    return coefficients.transpose(2, 3, 0, 1, 4).reshape(scale_count, 2 * channels, time_span)


def pair_sums(coefficients, first_flat, second_flat):
    scale_count = coefficients.shape[0]
    channels = coefficients.shape[1] // 2
    time_span = coefficients.shape[2]
    chan_iota = jnp.arange(channels, dtype=jnp.int32)
    both = jnp.concatenate([first_flat, second_flat])
    pick = (both[:, None] == chan_iota[None, :]).astype(jnp.bfloat16)
    parts = coefficients.reshape(scale_count, 2, channels, time_span)
    picked = jnp.einsum("pc,qrct->qrpt", pick, parts, preferred_element_type=jnp.float32)
    picked = picked.astype(jnp.bfloat16).astype(jnp.float32)
    pairs = first_flat.shape[0]
    first_real = picked[:, 0, :pairs]
    first_imag = picked[:, 1, :pairs]
    second_real = picked[:, 0, pairs:]
    second_imag = picked[:, 1, pairs:]
    cross_real = jnp.sum(first_real * second_real + first_imag * second_imag, axis=-1)
    cross_imag = jnp.sum(first_imag * second_real - first_real * second_imag, axis=-1)
    power_first = jnp.sum(first_real * first_real + first_imag * first_imag, axis=-1)
    power_second = jnp.sum(second_real * second_real + second_imag * second_imag, axis=-1)
    return jnp.stack([cross_real, cross_imag, power_first, power_second], axis=1)


def shards(signal, support, pair_first, pair_second, pair_count):
    groups = lax.axis_size("chan")
    cluster_number = lax.axis_index("chan")
    time_index = lax.axis_index("tm")
    time_devices = lax.axis_size("tm")
    time_span = signal.shape[1]
    ntime = time_span * time_devices
    rounded = signal.astype(jnp.bfloat16)
    near = jnp.concatenate(
        [from_behind(rounded, "tm", 1), rounded, from_behind(rounded, "tm", -1)], axis=1
    )
    wide = jnp.concatenate([from_behind(near, "tm", 3), near, from_behind(near, "tm", -3)], axis=1)
    extended = lax.all_gather(wide, "chan", axis=0, tiled=True)
    per_group = NS // groups
    scale_ids = cluster_number * per_group + jnp.arange(per_group, dtype=jnp.int32)
    coefficients = wavelet_band(
        extended, scale_ids, support[scale_ids], 4 * time_span // BLK, time_span
    )
    owner_devices, slots_total = pair_first.shape
    slots_local = slots_total // time_devices

    def by_block(pairs):
        return pairs.reshape(owner_devices, time_devices, slots_local).transpose(1, 0, 2).reshape(-1)

    sums = pair_sums(coefficients, by_block(pair_first), by_block(pair_second))
    values = sums.shape[1]
    partial_value = sums.transpose(2, 0, 1).reshape(time_devices, -1)
    exchanged = lax.all_to_all(partial_value, "tm", 0, 0, tiled=True)
    summed = jnp.sum(exchanged, axis=0).reshape(owner_devices, slots_local, per_group, values)
    owned = lax.all_to_all(summed, "chan", 0, 2, tiled=True)[0].transpose(0, 2, 1) / ntime
    slot_index = time_index * slots_local + jnp.arange(slots_local, dtype=jnp.int32)
    alive_mask = slot_index < pair_count[cluster_number]
    cross_real = owned[:, 0, :]
    cross_imag = owned[:, 1, :]
    first_power = owned[:, 2, :]
    second_power = owned[:, 3, :]
    coherence = (cross_real * cross_real + cross_imag * cross_imag) / (
        (first_power + power_floor) * (second_power + power_floor)
    )
    coherence = jnp.where(alive_mask[:, None], coherence, 0.0)[None]
    cross = jnp.stack([cross_real, cross_imag], axis=1)
    cross = jnp.where(alive_mask[:, None, None], cross, 0.0)[None]
    return (cross, coherence.astype(jnp.float32))


def solution(mesh):
    in_specs = (P("chan", "tm"), P(), P(), P(), P())
    out_specs = (P("chan", "tm", None, None), P("chan", "tm", None))
    return jax.shard_map(shards, mesh=mesh, in_specs=in_specs, out_specs=out_specs, check_vma=False)
```

```python
import math

import jax
import jax.numpy as jnp
import numpy as np
from jax import lax
from jax.experimental import pallas as pl
from jax.sharding import PartitionSpec as P

NS = 32
BLK = 128
TD = 128


power_floor = 1e-06


def from_behind(array, axis, by):
    peers = lax.axis_size(axis)
    return lax.ppermute(array, axis, [(i, (i + by) % peers) for i in range(peers)])


def kernel_table(scale_ids, reaches, offsets):
    taps = (2 * offsets + 1) * BLK
    lag = jnp.arange(taps, dtype=jnp.int32) - offsets * BLK
    within = jnp.arange(BLK, dtype=jnp.int32)
    scale_width = 2.0 * TD * jnp.exp2((scale_ids - (NS - 1)).astype(jnp.float32) / 4.0)
    offset = lag[:, None, None] - within[None, None, :]
    scaled_offset = offset.astype(jnp.float32) / scale_width[None, :, None]
    amplitude = (
        math.pi ** (-0.25)
        * lax.rsqrt(scale_width)[None, :, None]
        * jnp.exp(-0.5 * scaled_offset * scaled_offset)
    )
    inside = jnp.abs(offset) < (reaches * BLK)[None, :, None]
    lag_phase = 6.0 * (lag.astype(jnp.float32)[:, None] / scale_width[None, :])
    time_phase = 6.0 * (within.astype(jnp.float32)[None, :] / scale_width[:, None])
    lag_cos = jnp.cos(lag_phase)[:, :, None]
    lag_sin = jnp.sin(lag_phase)[:, :, None]
    time_cos = jnp.cos(time_phase)[None]
    time_sin = jnp.sin(time_phase)[None]
    cos_part = lag_cos * time_cos + lag_sin * time_sin
    sin_part = lag_sin * time_cos - lag_cos * time_sin
    real_part = jnp.where(inside, amplitude * cos_part, 0.0).astype(jnp.bfloat16)
    imag_part = jnp.where(inside, amplitude * sin_part, 0.0).astype(jnp.bfloat16)
    table = jnp.stack([real_part, imag_part], axis=2)
    return table.reshape(taps, -1)


def pair_kernel(coef_ref, pick_ref, out_ref):
    coef = coef_ref[...]
    first = jnp.dot(pick_ref[0], coef, preferred_element_type=jnp.float32)
    second = jnp.dot(pick_ref[1], coef, preferred_element_type=jnp.float32).astype(jnp.bfloat16)
    half = first.shape[1] // 2
    turned = jnp.concatenate([first[:, half:], -first[:, :half]], axis=1).astype(jnp.bfloat16)
    first = first.astype(jnp.bfloat16)
    size = first.shape[0]
    eye = lax.broadcasted_iota(jnp.int32, (size, size), 0) == lax.broadcasted_iota(
        jnp.int32, (size, size), 1
    )

    def diagonal(left, right):
        gram = lax.dot_general(
            left, right, (((1,), (1,)), ((), ())), preferred_element_type=jnp.float32
        )
        return jnp.sum(jnp.where(eye, gram, 0.0), axis=0, keepdims=True)

    out_ref[0, 0:1, :] = diagonal(first, second)
    out_ref[0, 1:2, :] = diagonal(turned, second)
    out_ref[0, 2:3, :] = diagonal(first, first)
    out_ref[0, 3:4, :] = diagonal(second, second)


def pair_sums(coefficients, first_flat, second_flat, scale_count):
    channels = coefficients.shape[0]
    width = coefficients.shape[1] // scale_count
    pairs = first_flat.shape[0]
    chan_iota = jnp.arange(channels, dtype=jnp.int32)
    both = jnp.stack([first_flat, second_flat])
    pick = (both[:, :, None] == chan_iota[None, None, :]).astype(jnp.bfloat16)
    block = 128
    return pl.pallas_call(
        pair_kernel,
        grid=(pairs // block, scale_count),
        in_specs=[
            pl.BlockSpec((channels, width), lambda b, q: (0, q)),
            pl.BlockSpec((2, block, channels), lambda b, q: (0, b, 0)),
        ],
        out_specs=pl.BlockSpec((1, 4, block), lambda b, q: (q, 0, b)),
        out_shape=jax.ShapeDtypeStruct((scale_count, 4, pairs), jnp.float32),
    )(coefficients, pick)


def shards(signal, support, pair_first, pair_second, pair_count):
    groups = lax.axis_size("chan")
    cluster_number = lax.axis_index("chan")
    time_index = lax.axis_index("tm")
    time_devices = lax.axis_size("tm")
    time_span = signal.shape[1]
    ntime = time_span * time_devices
    rounded = signal.astype(jnp.bfloat16)
    near = jnp.concatenate(
        [from_behind(rounded, "tm", 1), rounded, from_behind(rounded, "tm", -1)], axis=1
    )
    wide = jnp.concatenate([from_behind(near, "tm", 3), near, from_behind(near, "tm", -3)], axis=1)
    extended = lax.all_gather(wide, "chan", axis=0, tiled=True)
    per_group = NS // groups
    scale_ids = cluster_number * per_group + jnp.arange(per_group, dtype=jnp.int32)
    table = kernel_table(scale_ids, support[scale_ids], 4)
    coefficients = jnp.dot(extended, table, preferred_element_type=jnp.float32)
    coefficients = coefficients.astype(jnp.bfloat16)
    owner_devices, slots_total = pair_first.shape
    slots_local = slots_total // time_devices

    def by_block(pairs):
        return pairs.reshape(owner_devices, time_devices, slots_local).transpose(1, 0, 2).reshape(-1)

    sums = pair_sums(coefficients, by_block(pair_first), by_block(pair_second), per_group)
    values = sums.shape[1]
    chunk = owner_devices * slots_local
    partial_value = sums.reshape(per_group * values, time_devices, chunk).transpose(1, 0, 2)
    exchanged = lax.all_to_all(partial_value.reshape(time_devices, -1), "tm", 0, 0, tiled=True)
    summed = jnp.sum(exchanged, axis=0).reshape(per_group, values, owner_devices, slots_local)
    owned = lax.all_to_all(summed, "chan", 2, 0, tiled=True)[:, :, 0, :] / ntime
    slot_index = time_index * slots_local + jnp.arange(slots_local, dtype=jnp.int32)
    alive_mask = slot_index < pair_count[cluster_number]
    cross_real = owned[:, 0, :].T
    cross_imag = owned[:, 1, :].T
    first_power = owned[:, 2, :].T
    second_power = owned[:, 3, :].T
    coherence = (cross_real * cross_real + cross_imag * cross_imag) / (
        (first_power + power_floor) * (second_power + power_floor)
    )
    coherence = jnp.where(alive_mask[:, None], coherence, 0.0)[None]
    cross = jnp.stack([cross_real, cross_imag], axis=1)
    cross = jnp.where(alive_mask[:, None, None], cross, 0.0)[None]
    return (cross, coherence.astype(jnp.float32))


def solution(mesh):
    in_specs = (P("chan", "tm"), P(), P(), P(), P())
    out_specs = (P("chan", "tm", None, None), P("chan", "tm", None))
    return jax.shard_map(shards, mesh=mesh, in_specs=in_specs, out_specs=out_specs, check_vma=False)
```

```python
import math

import jax
import jax.numpy as jnp
import numpy as np
from jax import lax
from jax.sharding import PartitionSpec as P

NS = 32
BLK = 128
TD = 128


power_floor = 1e-06


def from_behind(array, axis, by):
    peers = lax.axis_size(axis)
    return lax.ppermute(array, axis, [(i, (i + by) % peers) for i in range(peers)])


def kernel_table(scale_ids, reaches, offsets):
    taps = (2 * offsets + 1) * BLK
    lag = jnp.arange(taps, dtype=jnp.int32) - offsets * BLK
    within = jnp.arange(BLK, dtype=jnp.int32)
    scale_width = 2.0 * TD * jnp.exp2((scale_ids - (NS - 1)).astype(jnp.float32) / 4.0)
    offset = lag[:, None, None] - within[None, None, :]
    scaled_offset = offset.astype(jnp.float32) / scale_width[None, :, None]
    amplitude = (
        math.pi ** (-0.25)
        * lax.rsqrt(scale_width)[None, :, None]
        * jnp.exp(-0.5 * scaled_offset * scaled_offset)
    )
    inside = jnp.abs(offset) < (reaches * BLK)[None, :, None]
    lag_phase = 6.0 * (lag.astype(jnp.float32)[:, None] / scale_width[None, :])
    time_phase = 6.0 * (within.astype(jnp.float32)[None, :] / scale_width[:, None])
    lag_cos = jnp.cos(lag_phase)[:, :, None]
    lag_sin = jnp.sin(lag_phase)[:, :, None]
    time_cos = jnp.cos(time_phase)[None]
    time_sin = jnp.sin(time_phase)[None]
    cos_part = lag_cos * time_cos + lag_sin * time_sin
    sin_part = lag_sin * time_cos - lag_cos * time_sin
    real_part = jnp.where(inside, amplitude * cos_part, 0.0).astype(jnp.bfloat16)
    imag_part = jnp.where(inside, amplitude * sin_part, 0.0).astype(jnp.bfloat16)
    table = jnp.stack([real_part, imag_part], axis=2)
    return table.reshape(taps, -1)


def pair_sums(coefficients, first_flat, second_flat, scale_count):
    channels = coefficients.shape[0]
    width = coefficients.shape[1] // scale_count
    pairs = first_flat.shape[0]
    chan_iota = jnp.arange(channels, dtype=jnp.int32)
    both = jnp.concatenate([first_flat, second_flat])
    pick = (both[:, None] == chan_iota[None, :]).astype(jnp.bfloat16)
    picked = jnp.dot(pick, coefficients, preferred_element_type=jnp.bfloat16)
    picked = picked.astype(jnp.float32).reshape(2, pairs, scale_count, 2, width // 2)
    first_real = picked[0, :, :, 0]
    first_imag = picked[0, :, :, 1]
    second_real = picked[1, :, :, 0]
    second_imag = picked[1, :, :, 1]
    cross_real = jnp.sum(first_real * second_real + first_imag * second_imag, axis=-1)
    cross_imag = jnp.sum(first_imag * second_real - first_real * second_imag, axis=-1)
    power_first = jnp.sum(first_real * first_real + first_imag * first_imag, axis=-1)
    power_second = jnp.sum(second_real * second_real + second_imag * second_imag, axis=-1)
    return jnp.stack([cross_real, cross_imag, power_first, power_second], axis=-1)


def shards(signal, support, pair_first, pair_second, pair_count):
    groups = lax.axis_size("chan")
    cluster_number = lax.axis_index("chan")
    time_index = lax.axis_index("tm")
    time_devices = lax.axis_size("tm")
    time_span = signal.shape[1]
    ntime = time_span * time_devices
    rounded = signal.astype(jnp.bfloat16)
    near = jnp.concatenate(
        [from_behind(rounded, "tm", 1), rounded, from_behind(rounded, "tm", -1)], axis=1
    )
    wide = jnp.concatenate([from_behind(near, "tm", 3), near, from_behind(near, "tm", -3)], axis=1)
    extended = lax.all_gather(wide, "chan", axis=0, tiled=True)
    per_group = NS // groups
    scale_ids = cluster_number * per_group + jnp.arange(per_group, dtype=jnp.int32)
    table = kernel_table(scale_ids, support[scale_ids], 4)
    coefficients = jnp.dot(extended, table, preferred_element_type=jnp.float32)
    coefficients = coefficients.astype(jnp.bfloat16)
    owner_devices, slots_total = pair_first.shape
    slots_local = slots_total // time_devices

    def by_block(pairs):
        return pairs.reshape(owner_devices, time_devices, slots_local).transpose(1, 0, 2).reshape(-1)

    sums = pair_sums(coefficients, by_block(pair_first), by_block(pair_second), per_group)
    values = sums.shape[-1]
    exchanged = lax.all_to_all(sums.reshape(time_devices, -1), "tm", 0, 0, tiled=True)
    summed = jnp.sum(exchanged, axis=0).reshape(owner_devices, slots_local, per_group, values)
    owned = lax.all_to_all(summed, "chan", 0, 2, tiled=True)[0] / ntime
    slot_index = time_index * slots_local + jnp.arange(slots_local, dtype=jnp.int32)
    alive_mask = slot_index < pair_count[cluster_number]
    cross_real = owned[:, :, 0]
    cross_imag = owned[:, :, 1]
    first_power = owned[:, :, 2]
    second_power = owned[:, :, 3]
    coherence = (cross_real * cross_real + cross_imag * cross_imag) / (
        (first_power + power_floor) * (second_power + power_floor)
    )
    coherence = jnp.where(alive_mask[:, None], coherence, 0.0)[None]
    cross = jnp.stack([cross_real, cross_imag], axis=1)
    cross = jnp.where(alive_mask[:, None, None], cross, 0.0)[None]
    return (cross, coherence.astype(jnp.float32))


def solution(mesh):
    in_specs = (P("chan", "tm"), P(), P(), P(), P())
    out_specs = (P("chan", "tm", None, None), P("chan", "tm", None))
    return jax.shard_map(shards, mesh=mesh, in_specs=in_specs, out_specs=out_specs, check_vma=False)
```

```python
import math

import jax
import jax.numpy as jnp
import numpy as np
from jax import lax
from jax.sharding import PartitionSpec as P

NS = 32
BLK = 128
TD = 128


power_floor = 1e-06


def from_behind(array, axis, by):
    peers = lax.axis_size(axis)
    return lax.ppermute(array, axis, [(i, (i + by) % peers) for i in range(peers)])


def kernel_table(scale_ids, reaches, offsets):
    taps = (2 * offsets + 1) * BLK
    lag = jnp.arange(taps, dtype=jnp.int32) - offsets * BLK
    within = jnp.arange(BLK, dtype=jnp.int32)
    scale_width = 2.0 * TD * jnp.exp2((scale_ids - (NS - 1)).astype(jnp.float32) / 4.0)
    offset = lag[:, None, None] - within[None, None, :]
    scaled_offset = offset.astype(jnp.float32) / scale_width[None, :, None]
    amplitude = (
        math.pi ** (-0.25)
        * lax.rsqrt(scale_width)[None, :, None]
        * jnp.exp(-0.5 * scaled_offset * scaled_offset)
    )
    inside = jnp.abs(offset) < (reaches * BLK)[None, :, None]
    lag_phase = 6.0 * (lag.astype(jnp.float32)[:, None] / scale_width[None, :])
    time_phase = 6.0 * (within.astype(jnp.float32)[None, :] / scale_width[:, None])
    lag_cos = jnp.cos(lag_phase)[:, :, None]
    lag_sin = jnp.sin(lag_phase)[:, :, None]
    time_cos = jnp.cos(time_phase)[None]
    time_sin = jnp.sin(time_phase)[None]
    cos_part = lag_cos * time_cos + lag_sin * time_sin
    sin_part = lag_sin * time_cos - lag_cos * time_sin
    real_part = jnp.where(inside, amplitude * cos_part, 0.0).astype(jnp.bfloat16)
    imag_part = jnp.where(inside, amplitude * sin_part, 0.0).astype(jnp.bfloat16)
    table = jnp.stack([real_part, imag_part], axis=2)
    return table.reshape(taps, -1)


def wavelet_band(extended, scale_ids, reaches, offsets, time_span):
    channels = extended.shape[0]
    blocks = time_span // BLK
    centre = 4 * time_span // BLK
    tap_blocks = 2 * offsets + 1
    pieces = [
        extended[:, (centre + offset_step) * BLK : (centre + offset_step) * BLK + time_span]
        for offset_step in range(-offsets, offsets + 1)
    ]
    unfolded = jnp.stack(pieces, axis=1).reshape(channels, tap_blocks, blocks, BLK)
    unfolded = unfolded.transpose(0, 2, 1, 3).reshape(channels * blocks, tap_blocks * BLK)
    table = kernel_table(scale_ids, reaches, offsets)
    coefficients = jnp.dot(unfolded, table, preferred_element_type=jnp.float32)
    scale_count = scale_ids.shape[0]
    coefficients = coefficients.astype(jnp.bfloat16).reshape(channels, blocks, scale_count, 2, BLK)
    return coefficients.transpose(2, 3, 0, 1, 4).reshape(scale_count, 2 * channels, time_span)


def pair_sums(coefficients, first_flat, second_flat):
    scale_count = coefficients.shape[0]
    channels = coefficients.shape[1] // 2
    time_span = coefficients.shape[2]
    chan_iota = jnp.arange(channels, dtype=jnp.int32)
    both = jnp.concatenate([first_flat, second_flat])
    pick = (both[:, None] == chan_iota[None, :]).astype(jnp.bfloat16)
    parts = coefficients.reshape(scale_count, 2, channels, time_span)
    picked = jnp.einsum("pc,qrct->qrpt", pick, parts, preferred_element_type=jnp.bfloat16)
    pairs = first_flat.shape[0]
    first_real = picked[:, 0, :pairs]
    first_imag = picked[:, 1, :pairs]
    second_real = picked[:, 0, pairs:]
    second_imag = picked[:, 1, pairs:]

    def time_sum(left, right):
        return jnp.einsum("qpt,qpt->qp", left, right, preferred_element_type=jnp.float32)

    cross_real = time_sum(first_real, second_real) + time_sum(first_imag, second_imag)
    cross_imag = time_sum(first_imag, second_real) - time_sum(first_real, second_imag)
    power_first = time_sum(first_real, first_real) + time_sum(first_imag, first_imag)
    power_second = time_sum(second_real, second_real) + time_sum(second_imag, second_imag)
    return jnp.stack([cross_real, cross_imag, power_first, power_second], axis=1)


def shards(signal, support, pair_first, pair_second, pair_count):
    groups = lax.axis_size("chan")
    cluster_number = lax.axis_index("chan")
    time_index = lax.axis_index("tm")
    time_devices = lax.axis_size("tm")
    time_span = signal.shape[1]
    ntime = time_span * time_devices
    rounded = signal.astype(jnp.bfloat16)
    near = jnp.concatenate(
        [from_behind(rounded, "tm", 1), rounded, from_behind(rounded, "tm", -1)], axis=1
    )
    wide = jnp.concatenate([from_behind(near, "tm", 3), near, from_behind(near, "tm", -3)], axis=1)
    extended = lax.all_gather(wide, "chan", axis=0, tiled=True)
    per_group = NS // groups
    scale_ids = cluster_number * per_group + jnp.arange(per_group, dtype=jnp.int32)
    coefficients = wavelet_band(
        extended, scale_ids, support[scale_ids], 4 * time_span // BLK, time_span
    )
    owner_devices, slots_total = pair_first.shape
    slots_local = slots_total // time_devices

    def by_block(pairs):
        return pairs.reshape(owner_devices, time_devices, slots_local).transpose(1, 0, 2).reshape(-1)

    sums = pair_sums(coefficients, by_block(pair_first), by_block(pair_second))
    values = sums.shape[1]
    chunk = owner_devices * slots_local
    partial_value = sums.reshape(per_group * values, time_devices, chunk).transpose(1, 0, 2)
    exchanged = lax.all_to_all(partial_value.reshape(time_devices, -1), "tm", 0, 0, tiled=True)
    summed = jnp.sum(exchanged, axis=0).reshape(per_group, values, owner_devices, slots_local)
    owned = lax.all_to_all(summed, "chan", 2, 0, tiled=True)[:, :, 0, :] / ntime
    slot_index = time_index * slots_local + jnp.arange(slots_local, dtype=jnp.int32)
    alive_mask = slot_index < pair_count[cluster_number]
    cross_real = owned[:, 0, :].T
    cross_imag = owned[:, 1, :].T
    first_power = owned[:, 2, :].T
    second_power = owned[:, 3, :].T
    coherence = (cross_real * cross_real + cross_imag * cross_imag) / (
        (first_power + power_floor) * (second_power + power_floor)
    )
    coherence = jnp.where(alive_mask[:, None], coherence, 0.0)[None]
    cross = jnp.stack([cross_real, cross_imag], axis=1)
    cross = jnp.where(alive_mask[:, None, None], cross, 0.0)[None]
    return (cross, coherence.astype(jnp.float32))


def solution(mesh):
    in_specs = (P("chan", "tm"), P(), P(), P(), P())
    out_specs = (P("chan", "tm", None, None), P("chan", "tm", None))
    return jax.shard_map(shards, mesh=mesh, in_specs=in_specs, out_specs=out_specs, check_vma=False)
```

```python
import math

import jax
import jax.numpy as jnp
import numpy as np
from jax import lax
from jax.sharding import PartitionSpec as P

NS = 32
BLK = 128
TD = 128


power_floor = 1e-06


def from_behind(array, axis, by):
    peers = lax.axis_size(axis)
    return lax.ppermute(array, axis, [(i, (i + by) % peers) for i in range(peers)])


def kernel_table(scale_ids, reaches, offsets):
    taps = (2 * offsets + 1) * BLK
    lag = jnp.arange(taps, dtype=jnp.int32) - offsets * BLK
    within = jnp.arange(BLK, dtype=jnp.int32)
    scale_width = 2.0 * TD * jnp.exp2((scale_ids - (NS - 1)).astype(jnp.float32) / 4.0)
    offset = lag[:, None, None] - within[None, None, :]
    scaled_offset = offset.astype(jnp.float32) / scale_width[None, :, None]
    amplitude = (
        math.pi ** (-0.25)
        * lax.rsqrt(scale_width)[None, :, None]
        * jnp.exp(-0.5 * scaled_offset * scaled_offset)
    )
    inside = jnp.abs(offset) < (reaches * BLK)[None, :, None]
    lag_phase = 6.0 * (lag.astype(jnp.float32)[:, None] / scale_width[None, :])
    time_phase = 6.0 * (within.astype(jnp.float32)[None, :] / scale_width[:, None])
    lag_cos = jnp.cos(lag_phase)[:, :, None]
    lag_sin = jnp.sin(lag_phase)[:, :, None]
    time_cos = jnp.cos(time_phase)[None]
    time_sin = jnp.sin(time_phase)[None]
    cos_part = lag_cos * time_cos + lag_sin * time_sin
    sin_part = lag_sin * time_cos - lag_cos * time_sin
    real_part = jnp.where(inside, amplitude * cos_part, 0.0).astype(jnp.bfloat16)
    imag_part = jnp.where(inside, amplitude * sin_part, 0.0).astype(jnp.bfloat16)
    table = jnp.stack([real_part, imag_part], axis=2)
    return table.reshape(taps, -1)


def wavelet_band(extended, scale_ids, reaches, offsets, time_span):
    channels = extended.shape[0]
    blocks = time_span // BLK
    centre = 4 * time_span // BLK
    tap_blocks = 2 * offsets + 1
    pieces = [
        extended[:, (centre + offset_step) * BLK : (centre + offset_step) * BLK + time_span]
        for offset_step in range(-offsets, offsets + 1)
    ]
    unfolded = jnp.stack(pieces, axis=1).reshape(channels, tap_blocks, blocks, BLK)
    unfolded = unfolded.transpose(0, 2, 1, 3).reshape(channels * blocks, tap_blocks * BLK)
    table = kernel_table(scale_ids, reaches, offsets)
    coefficients = jnp.dot(unfolded, table, preferred_element_type=jnp.float32)
    scale_count = scale_ids.shape[0]
    coefficients = coefficients.astype(jnp.bfloat16).reshape(channels, blocks, scale_count, 2, BLK)
    return coefficients.transpose(2, 3, 0, 1, 4).reshape(scale_count, 2 * channels, time_span)


def pair_sums(coefficients, first_flat, second_flat):
    scale_count = coefficients.shape[0]
    channels = coefficients.shape[1] // 2
    time_span = coefficients.shape[2]
    chan_iota = jnp.arange(channels, dtype=jnp.int32)
    both = jnp.concatenate([first_flat, second_flat])
    pick = (both[:, None] == chan_iota[None, :]).astype(jnp.bfloat16)
    parts = coefficients.reshape(scale_count, 2, channels, time_span)
    picked = jnp.einsum("pc,qrct->qrpt", pick, parts, preferred_element_type=jnp.bfloat16)
    pairs = first_flat.shape[0]
    first_real = picked[:, 0, :pairs]
    first_imag = picked[:, 1, :pairs]
    second_real = picked[:, 0, pairs:]
    second_imag = picked[:, 1, pairs:]

    def time_sum(left, right):
        return jnp.einsum("qpt,qpt->qp", left, right, preferred_element_type=jnp.float32)

    cross_real = time_sum(first_real, second_real) + time_sum(first_imag, second_imag)
    cross_imag = time_sum(first_imag, second_real) - time_sum(first_real, second_imag)
    power_first = time_sum(first_real, first_real) + time_sum(first_imag, first_imag)
    power_second = time_sum(second_real, second_real) + time_sum(second_imag, second_imag)
    return jnp.stack([cross_real, cross_imag, power_first, power_second], axis=1)


def shards(signal, support, pair_first, pair_second, pair_count):
    groups = lax.axis_size("chan")
    cluster_number = lax.axis_index("chan")
    time_index = lax.axis_index("tm")
    time_devices = lax.axis_size("tm")
    time_span = signal.shape[1]
    ntime = time_span * time_devices
    rounded = signal.astype(jnp.bfloat16)
    near = jnp.concatenate(
        [from_behind(rounded, "tm", 1), rounded, from_behind(rounded, "tm", -1)], axis=1
    )
    wide = jnp.concatenate([from_behind(near, "tm", 3), near, from_behind(near, "tm", -3)], axis=1)
    extended = lax.all_gather(wide, "chan", axis=0, tiled=True)
    per_group = NS // groups
    scale_ids = cluster_number * per_group + jnp.arange(per_group, dtype=jnp.int32)
    coefficients = wavelet_band(
        extended, scale_ids, support[scale_ids], 4 * time_span // BLK, time_span
    )
    owner_devices, slots_total = pair_first.shape
    slots_local = slots_total // time_devices

    def by_block(pairs):
        return pairs.reshape(owner_devices, time_devices, slots_local).transpose(1, 0, 2).reshape(-1)

    sums = pair_sums(coefficients, by_block(pair_first), by_block(pair_second))
    values = sums.shape[1]
    chunk = owner_devices * slots_local
    partial_value = sums.reshape(per_group * values, time_devices, chunk).transpose(1, 0, 2)
    inner = 8
    outer = time_devices // inner
    near_groups = [[o * inner + i for i in range(inner)] for o in range(outer)]
    far_groups = [[o * inner + i for o in range(outer)] for i in range(inner)]
    staged = partial_value.reshape(outer, inner, -1).transpose(1, 0, 2)
    staged = lax.all_to_all(staged, "tm", 0, 0, axis_index_groups=near_groups, tiled=True)
    staged = jnp.sum(staged.reshape(inner, outer, -1), axis=0)
    exchanged = lax.all_to_all(staged, "tm", 0, 0, axis_index_groups=far_groups, tiled=True)
    summed = jnp.sum(exchanged, axis=0).reshape(per_group, values, owner_devices, slots_local)
    owned = lax.all_to_all(summed, "chan", 2, 0, tiled=True)[:, :, 0, :] / ntime
    slot_index = time_index * slots_local + jnp.arange(slots_local, dtype=jnp.int32)
    alive_mask = slot_index < pair_count[cluster_number]
    cross_real = owned[:, 0, :].T
    cross_imag = owned[:, 1, :].T
    first_power = owned[:, 2, :].T
    second_power = owned[:, 3, :].T
    coherence = (cross_real * cross_real + cross_imag * cross_imag) / (
        (first_power + power_floor) * (second_power + power_floor)
    )
    coherence = jnp.where(alive_mask[:, None], coherence, 0.0)[None]
    cross = jnp.stack([cross_real, cross_imag], axis=1)
    cross = jnp.where(alive_mask[:, None, None], cross, 0.0)[None]
    return (cross, coherence.astype(jnp.float32))


def solution(mesh):
    in_specs = (P("chan", "tm"), P(), P(), P(), P())
    out_specs = (P("chan", "tm", None, None), P("chan", "tm", None))
    return jax.shard_map(shards, mesh=mesh, in_specs=in_specs, out_specs=out_specs, check_vma=False)
```

```python
import math

import jax
import jax.numpy as jnp
import numpy as np
from jax import lax
from jax.sharding import PartitionSpec as P

NS = 32
BLK = 128
TD = 128


power_floor = 1e-06


def from_behind(array, axis, by):
    peers = lax.axis_size(axis)
    return lax.ppermute(array, axis, [(i, (i + by) % peers) for i in range(peers)])


def kernel_table(scale_ids, reaches, offsets):
    taps = (2 * offsets + 1) * BLK
    lag = jnp.arange(taps, dtype=jnp.int32) - offsets * BLK
    within = jnp.arange(BLK, dtype=jnp.int32)
    scale_width = 2.0 * TD * jnp.exp2((scale_ids - (NS - 1)).astype(jnp.float32) / 4.0)
    offset = lag[:, None, None] - within[None, None, :]
    scaled_offset = offset.astype(jnp.float32) / scale_width[None, :, None]
    amplitude = (
        math.pi ** (-0.25)
        * lax.rsqrt(scale_width)[None, :, None]
        * jnp.exp(-0.5 * scaled_offset * scaled_offset)
    )
    inside = jnp.abs(offset) < (reaches * BLK)[None, :, None]
    lag_phase = 6.0 * (lag.astype(jnp.float32)[:, None] / scale_width[None, :])
    time_phase = 6.0 * (within.astype(jnp.float32)[None, :] / scale_width[:, None])
    lag_cos = jnp.cos(lag_phase)[:, :, None]
    lag_sin = jnp.sin(lag_phase)[:, :, None]
    time_cos = jnp.cos(time_phase)[None]
    time_sin = jnp.sin(time_phase)[None]
    cos_part = lag_cos * time_cos + lag_sin * time_sin
    sin_part = lag_sin * time_cos - lag_cos * time_sin
    real_part = jnp.where(inside, amplitude * cos_part, 0.0).astype(jnp.bfloat16)
    imag_part = jnp.where(inside, amplitude * sin_part, 0.0).astype(jnp.bfloat16)
    table = jnp.stack([real_part, imag_part], axis=2)
    return table.reshape(taps, -1)


def band_coefficients(extended, scale_ids, reaches, offsets):
    channels = extended.shape[0]
    table = kernel_table(scale_ids, reaches, offsets)
    coefficients = jnp.dot(extended, table, preferred_element_type=jnp.float32)
    scale_count = scale_ids.shape[0]
    coefficients = coefficients.astype(jnp.bfloat16).reshape(channels, scale_count, 2, BLK)
    return coefficients.transpose(1, 2, 0, 3).reshape(scale_count, 2 * channels, BLK)


def pair_sums(coefficients, first_flat, second_flat):
    scale_count = coefficients.shape[0]
    channels = coefficients.shape[1] // 2
    time_span = coefficients.shape[2]
    chan_iota = jnp.arange(channels, dtype=jnp.int32)
    both = jnp.concatenate([first_flat, second_flat])
    pick = (both[:, None] == chan_iota[None, :]).astype(jnp.bfloat16)
    parts = coefficients.reshape(scale_count, 2, channels, time_span)
    picked = jnp.einsum("pc,qrct->qrpt", pick, parts, preferred_element_type=jnp.bfloat16)
    pairs = first_flat.shape[0]
    first_real = picked[:, 0, :pairs]
    first_imag = picked[:, 1, :pairs]
    second_real = picked[:, 0, pairs:]
    second_imag = picked[:, 1, pairs:]

    def time_sum(left, right):
        return jnp.einsum("qpt,qpt->qp", left, right, preferred_element_type=jnp.float32)

    cross_real = time_sum(first_real, second_real) + time_sum(first_imag, second_imag)
    cross_imag = time_sum(first_imag, second_real) - time_sum(first_real, second_imag)
    power_first = time_sum(first_real, first_real) + time_sum(first_imag, first_imag)
    power_second = time_sum(second_real, second_real) + time_sum(second_imag, second_imag)
    return jnp.stack([cross_real, cross_imag, power_first, power_second], axis=1)


def shards(signal, support, pair_first, pair_second, pair_count):
    groups = lax.axis_size("chan")
    cluster_number = lax.axis_index("chan")
    time_index = lax.axis_index("tm")
    time_devices = lax.axis_size("tm")
    time_span = signal.shape[1]
    ntime = time_span * time_devices
    rounded = signal.astype(jnp.bfloat16)
    gathered = lax.all_gather(rounded, "chan", axis=0, tiled=True)
    near = jnp.concatenate(
        [from_behind(gathered, "tm", 1), gathered, from_behind(gathered, "tm", -1)], axis=1
    )
    wide = jnp.concatenate([from_behind(near, "tm", 3), near, from_behind(near, "tm", -3)], axis=1)
    per_group = NS // groups
    band = NS // 4
    narrow_count = (NS - band) // groups
    wide_count = band // groups
    narrow_ids = cluster_number * narrow_count + jnp.arange(narrow_count, dtype=jnp.int32)
    wide_ids = NS - band + cluster_number * wide_count + jnp.arange(wide_count, dtype=jnp.int32)
    narrow_coefficients = band_coefficients(near, narrow_ids, support[narrow_ids], 1)
    wide_coefficients = band_coefficients(wide, wide_ids, support[wide_ids], 4)
    owner_devices, slots_total = pair_first.shape
    slots_local = slots_total // time_devices

    def by_block(pairs):
        return pairs.reshape(owner_devices, time_devices, slots_local).transpose(1, 0, 2).reshape(-1)

    first_flat = by_block(pair_first)
    second_flat = by_block(pair_second)
    sums = jnp.concatenate(
        [
            pair_sums(narrow_coefficients, first_flat, second_flat),
            pair_sums(wide_coefficients, first_flat, second_flat),
        ],
        axis=0,
    )
    values = sums.shape[1]
    chunk = owner_devices * slots_local
    partial_value = sums.reshape(per_group * values, time_devices, chunk).transpose(1, 0, 2)
    exchanged = lax.all_to_all(partial_value.reshape(time_devices, -1), "tm", 0, 0, tiled=True)
    summed = jnp.sum(exchanged, axis=0).reshape(per_group, values, owner_devices, slots_local)
    owned = lax.all_to_all(summed, "chan", 2, 0, tiled=True)[:, :, 0, :] / ntime
    owned = owned.reshape(groups, per_group, values, slots_local)
    owned = jnp.concatenate(
        [
            owned[:, :narrow_count].reshape(groups * narrow_count, values, slots_local),
            owned[:, narrow_count:].reshape(groups * wide_count, values, slots_local),
        ],
        axis=0,
    )
    slot_index = time_index * slots_local + jnp.arange(slots_local, dtype=jnp.int32)
    alive_mask = slot_index < pair_count[cluster_number]
    cross_real = owned[:, 0, :].T
    cross_imag = owned[:, 1, :].T
    first_power = owned[:, 2, :].T
    second_power = owned[:, 3, :].T
    coherence = (cross_real * cross_real + cross_imag * cross_imag) / (
        (first_power + power_floor) * (second_power + power_floor)
    )
    coherence = jnp.where(alive_mask[:, None], coherence, 0.0)[None]
    cross = jnp.stack([cross_real, cross_imag], axis=1)
    cross = jnp.where(alive_mask[:, None, None], cross, 0.0)[None]
    return (cross, coherence.astype(jnp.float32))


def solution(mesh):
    in_specs = (P("chan", "tm"), P(), P(), P(), P())
    out_specs = (P("chan", "tm", None, None), P("chan", "tm", None))
    return jax.shard_map(shards, mesh=mesh, in_specs=in_specs, out_specs=out_specs, check_vma=False)
```

```python
import math

import jax
import jax.numpy as jnp
import numpy as np
from jax import lax
from jax.sharding import PartitionSpec as P

NS = 32
BLK = 128
TD = 128


power_floor = 1e-06


def from_behind(array, axis, by):
    peers = lax.axis_size(axis)
    return lax.ppermute(array, axis, [(i, (i + by) % peers) for i in range(peers)])


def kernel_table(scale_ids, reaches, offsets):
    taps = (2 * offsets + 1) * BLK
    lag = jnp.arange(taps, dtype=jnp.int32) - offsets * BLK
    within = jnp.arange(BLK, dtype=jnp.int32)
    scale_width = 2.0 * TD * jnp.exp2((scale_ids - (NS - 1)).astype(jnp.float32) / 4.0)
    width = scale_width[:, None, None]
    offset = lag[None, :, None] - within[None, None, :]
    scaled_offset = offset.astype(jnp.float32) / width
    amplitude = math.pi ** (-0.25) * lax.rsqrt(width) * jnp.exp(-0.5 * scaled_offset * scaled_offset)
    inside = jnp.abs(offset) < (reaches * BLK)[:, None, None]
    lag_phase = 6.0 * (lag.astype(jnp.float32)[None, :] / scale_width[:, None])
    time_phase = 6.0 * (within.astype(jnp.float32)[None, :] / scale_width[:, None])
    lag_cos = jnp.cos(lag_phase)[:, :, None]
    lag_sin = jnp.sin(lag_phase)[:, :, None]
    time_cos = jnp.cos(time_phase)[:, None, :]
    time_sin = jnp.sin(time_phase)[:, None, :]
    cos_part = lag_cos * time_cos + lag_sin * time_sin
    sin_part = lag_sin * time_cos - lag_cos * time_sin
    real_part = jnp.where(inside, amplitude * cos_part, 0.0).astype(jnp.bfloat16)
    imag_part = jnp.where(inside, amplitude * sin_part, 0.0).astype(jnp.bfloat16)
    return jnp.stack([real_part, imag_part], axis=1)


def band_coefficients(extended, scale_ids, reaches, offsets):
    channels = extended.shape[0]
    table = kernel_table(scale_ids, reaches, offsets)
    coefficients = jnp.einsum("cm,qrmt->qrct", extended, table, preferred_element_type=jnp.float32)
    scale_count = scale_ids.shape[0]
    return coefficients.astype(jnp.bfloat16).reshape(scale_count, 2 * channels, BLK)


def pair_sums(coefficients, first_flat, second_flat):
    scale_count = coefficients.shape[0]
    channels = coefficients.shape[1] // 2
    time_span = coefficients.shape[2]
    chan_iota = jnp.arange(channels, dtype=jnp.int32)
    both = jnp.concatenate([first_flat, second_flat])
    pick = (both[:, None] == chan_iota[None, :]).astype(jnp.bfloat16)
    parts = coefficients.reshape(scale_count, 2, channels, time_span)
    picked = jnp.einsum("pc,qrct->qrpt", pick, parts, preferred_element_type=jnp.bfloat16)
    pairs = first_flat.shape[0]
    first_real = picked[:, 0, :pairs]
    first_imag = picked[:, 1, :pairs]
    second_real = picked[:, 0, pairs:]
    second_imag = picked[:, 1, pairs:]

    def time_sum(left, right):
        return jnp.einsum("qpt,qpt->qp", left, right, preferred_element_type=jnp.float32)

    cross_real = time_sum(first_real, second_real) + time_sum(first_imag, second_imag)
    cross_imag = time_sum(first_imag, second_real) - time_sum(first_real, second_imag)
    power_first = time_sum(first_real, first_real) + time_sum(first_imag, first_imag)
    power_second = time_sum(second_real, second_real) + time_sum(second_imag, second_imag)
    return jnp.stack([cross_real, cross_imag, power_first, power_second], axis=1)


def shards(signal, support, pair_first, pair_second, pair_count):
    groups = lax.axis_size("chan")
    cluster_number = lax.axis_index("chan")
    time_index = lax.axis_index("tm")
    time_devices = lax.axis_size("tm")
    time_span = signal.shape[1]
    ntime = time_span * time_devices
    rounded = signal.astype(jnp.bfloat16)
    gathered = lax.all_gather(rounded, "chan", axis=0, tiled=True)
    near = jnp.concatenate(
        [from_behind(gathered, "tm", 1), gathered, from_behind(gathered, "tm", -1)], axis=1
    )
    wide = jnp.concatenate([from_behind(near, "tm", 3), near, from_behind(near, "tm", -3)], axis=1)
    per_group = NS // groups
    band = NS // 4
    narrow_count = (NS - band) // groups
    wide_count = band // groups
    narrow_ids = cluster_number * narrow_count + jnp.arange(narrow_count, dtype=jnp.int32)
    wide_ids = NS - band + cluster_number * wide_count + jnp.arange(wide_count, dtype=jnp.int32)
    narrow_coefficients = band_coefficients(near, narrow_ids, support[narrow_ids], 1)
    wide_coefficients = band_coefficients(wide, wide_ids, support[wide_ids], 4)
    owner_devices, slots_total = pair_first.shape
    slots_local = slots_total // time_devices

    def by_block(pairs):
        return pairs.reshape(owner_devices, time_devices, slots_local).transpose(1, 0, 2).reshape(-1)

    first_flat = by_block(pair_first)
    second_flat = by_block(pair_second)
    sums = jnp.concatenate(
        [
            pair_sums(narrow_coefficients, first_flat, second_flat),
            pair_sums(wide_coefficients, first_flat, second_flat),
        ],
        axis=0,
    )
    values = sums.shape[1]
    chunk = owner_devices * slots_local
    partial_value = sums.reshape(per_group * values, time_devices, chunk).transpose(1, 0, 2)
    exchanged = lax.all_to_all(partial_value.reshape(time_devices, -1), "tm", 0, 0, tiled=True)
    summed = jnp.sum(exchanged, axis=0).reshape(per_group, values, owner_devices, slots_local)
    owned = lax.all_to_all(summed, "chan", 2, 0, tiled=True)[:, :, 0, :] / ntime
    owned = owned.reshape(groups, per_group, values, slots_local)
    owned = jnp.concatenate(
        [
            owned[:, :narrow_count].reshape(groups * narrow_count, values, slots_local),
            owned[:, narrow_count:].reshape(groups * wide_count, values, slots_local),
        ],
        axis=0,
    )
    slot_index = time_index * slots_local + jnp.arange(slots_local, dtype=jnp.int32)
    alive_mask = slot_index < pair_count[cluster_number]
    cross_real = owned[:, 0, :].T
    cross_imag = owned[:, 1, :].T
    first_power = owned[:, 2, :].T
    second_power = owned[:, 3, :].T
    coherence = (cross_real * cross_real + cross_imag * cross_imag) / (
        (first_power + power_floor) * (second_power + power_floor)
    )
    coherence = jnp.where(alive_mask[:, None], coherence, 0.0)[None]
    cross = jnp.stack([cross_real, cross_imag], axis=1)
    cross = jnp.where(alive_mask[:, None, None], cross, 0.0)[None]
    return (cross, coherence.astype(jnp.float32))


def solution(mesh):
    in_specs = (P("chan", "tm"), P(), P(), P(), P())
    out_specs = (P("chan", "tm", None, None), P("chan", "tm", None))
    return jax.shard_map(shards, mesh=mesh, in_specs=in_specs, out_specs=out_specs, check_vma=False)
```

```python
import math

import jax
import jax.numpy as jnp
import numpy as np
from jax import lax
from jax.sharding import PartitionSpec as P

NS = 32
BLK = 128
TD = 128


power_floor = 1e-06


def from_behind(array, axis, by):
    peers = lax.axis_size(axis)
    return lax.ppermute(array, axis, [(i, (i + by) % peers) for i in range(peers)])


def kernel_table(scale_ids, reaches, offsets):
    taps = (2 * offsets + 1) * BLK
    lag = jnp.arange(taps, dtype=jnp.int32) - offsets * BLK
    within = jnp.arange(BLK, dtype=jnp.int32)
    scale_width = 2.0 * TD * jnp.exp2((scale_ids - (NS - 1)).astype(jnp.float32) / 4.0)
    width = scale_width[:, None, None]
    offset = lag[None, :, None] - within[None, None, :]
    scaled_offset = offset.astype(jnp.float32) / width
    amplitude = math.pi ** (-0.25) * lax.rsqrt(width) * jnp.exp(-0.5 * scaled_offset * scaled_offset)
    inside = jnp.abs(offset) < (reaches * BLK)[:, None, None]
    lag_phase = 6.0 * (lag.astype(jnp.float32)[None, :] / scale_width[:, None])
    time_phase = 6.0 * (within.astype(jnp.float32)[None, :] / scale_width[:, None])
    lag_cos = jnp.cos(lag_phase)[:, :, None]
    lag_sin = jnp.sin(lag_phase)[:, :, None]
    time_cos = jnp.cos(time_phase)[:, None, :]
    time_sin = jnp.sin(time_phase)[:, None, :]
    cos_part = lag_cos * time_cos + lag_sin * time_sin
    sin_part = lag_sin * time_cos - lag_cos * time_sin
    real_part = jnp.where(inside, amplitude * cos_part, 0.0).astype(jnp.bfloat16)
    imag_part = jnp.where(inside, amplitude * sin_part, 0.0).astype(jnp.bfloat16)
    return jnp.stack([real_part, imag_part], axis=1)


def band_coefficients(extended, scale_ids, reaches, offsets):
    channels = extended.shape[0]
    table = kernel_table(scale_ids, reaches, offsets)
    coefficients = jnp.einsum("cm,qrmt->qrct", extended, table, preferred_element_type=jnp.float32)
    scale_count = scale_ids.shape[0]
    return coefficients.astype(jnp.bfloat16).reshape(scale_count, 2 * channels, BLK)


def pair_sums(coefficients, first_flat, second_flat):
    scale_count = coefficients.shape[0]
    channels = coefficients.shape[1] // 2
    time_span = coefficients.shape[2]
    chan_iota = jnp.arange(channels, dtype=jnp.int32)
    both = jnp.concatenate([first_flat, second_flat])
    pick = (both[:, None] == chan_iota[None, :]).astype(jnp.bfloat16)
    parts = coefficients.reshape(scale_count, 2, channels, time_span)
    picked = jnp.einsum("pc,qrct->qrpt", pick, parts, preferred_element_type=jnp.bfloat16)
    pairs = first_flat.shape[0]
    first_real = picked[:, 0, :pairs]
    first_imag = picked[:, 1, :pairs]
    second_real = picked[:, 0, pairs:]
    second_imag = picked[:, 1, pairs:]

    def time_sum(left, right):
        return jnp.einsum("qpt,qpt->qp", left, right, preferred_element_type=jnp.float32)

    cross_real = time_sum(first_real, second_real) + time_sum(first_imag, second_imag)
    cross_imag = time_sum(first_imag, second_real) - time_sum(first_real, second_imag)
    power_first = time_sum(first_real, first_real) + time_sum(first_imag, first_imag)
    power_second = time_sum(second_real, second_real) + time_sum(second_imag, second_imag)
    return jnp.stack([cross_real, cross_imag, power_first, power_second], axis=1)


def shards(signal, support, pair_first, pair_second, pair_count):
    groups = lax.axis_size("chan")
    cluster_number = lax.axis_index("chan")
    time_index = lax.axis_index("tm")
    time_devices = lax.axis_size("tm")
    time_span = signal.shape[1]
    ntime = time_span * time_devices
    rounded = signal.astype(jnp.bfloat16)
    gathered = lax.all_gather(rounded, "chan", axis=0, tiled=True)
    near = jnp.concatenate(
        [from_behind(gathered, "tm", 1), gathered, from_behind(gathered, "tm", -1)], axis=1
    )
    wide = jnp.concatenate([from_behind(near, "tm", 3), near, from_behind(near, "tm", -3)], axis=1)
    per_group = NS // groups
    band = NS // 4
    narrow_count = (NS - band) // groups
    wide_count = band // groups
    narrow_ids = cluster_number * narrow_count + jnp.arange(narrow_count, dtype=jnp.int32)
    wide_ids = NS - band + cluster_number * wide_count + jnp.arange(wide_count, dtype=jnp.int32)
    narrow_coefficients = band_coefficients(near, narrow_ids, support[narrow_ids], 1)
    wide_coefficients = band_coefficients(wide, wide_ids, support[wide_ids], 4)
    owner_devices, slots_total = pair_first.shape
    slots_local = slots_total // time_devices

    def by_block(pairs):
        return pairs.reshape(owner_devices, time_devices, slots_local).transpose(1, 0, 2).reshape(-1)

    first_flat = by_block(pair_first)
    second_flat = by_block(pair_second)
    sums = jnp.concatenate(
        [
            pair_sums(narrow_coefficients, first_flat, second_flat),
            pair_sums(wide_coefficients, first_flat, second_flat),
        ],
        axis=0,
    )
    values = sums.shape[1]
    destinations = time_devices * groups
    partial_value = sums.reshape(per_group * values, destinations, slots_local).transpose(1, 0, 2)
    exchanged = lax.all_to_all(
        partial_value.reshape(destinations, -1), ("tm", "chan"), 0, 0, tiled=True
    )
    exchanged = exchanged.reshape(time_devices, groups, per_group, values, slots_local)
    owned = jnp.sum(exchanged, axis=0) / ntime
    owned = owned.reshape(groups, per_group, values, slots_local)
    owned = jnp.concatenate(
        [
            owned[:, :narrow_count].reshape(groups * narrow_count, values, slots_local),
            owned[:, narrow_count:].reshape(groups * wide_count, values, slots_local),
        ],
        axis=0,
    )
    slot_index = time_index * slots_local + jnp.arange(slots_local, dtype=jnp.int32)
    alive_mask = slot_index < pair_count[cluster_number]
    cross_real = owned[:, 0, :].T
    cross_imag = owned[:, 1, :].T
    first_power = owned[:, 2, :].T
    second_power = owned[:, 3, :].T
    coherence = (cross_real * cross_real + cross_imag * cross_imag) / (
        (first_power + power_floor) * (second_power + power_floor)
    )
    coherence = jnp.where(alive_mask[:, None], coherence, 0.0)[None]
    cross = jnp.stack([cross_real, cross_imag], axis=1)
    cross = jnp.where(alive_mask[:, None, None], cross, 0.0)[None]
    return (cross, coherence.astype(jnp.float32))


def solution(mesh):
    in_specs = (P("chan", "tm"), P(), P(), P(), P())
    out_specs = (P("chan", "tm", None, None), P("chan", "tm", None))
    return jax.shard_map(shards, mesh=mesh, in_specs=in_specs, out_specs=out_specs, check_vma=False)
```

```python
import math

import jax
import jax.numpy as jnp
import numpy as np
from jax import lax
from jax.sharding import PartitionSpec as P

NS = 32
BLK = 128
TD = 128


power_floor = 1e-06


def from_behind(array, axis, by):
    peers = lax.axis_size(axis)
    return lax.ppermute(array, axis, [(i, (i + by) % peers) for i in range(peers)])


def kernel_table(scale_ids, reaches, offsets):
    taps = (2 * offsets + 1) * BLK
    lag = jnp.arange(taps, dtype=jnp.int32) - offsets * BLK
    within = jnp.arange(BLK, dtype=jnp.int32)
    scale_width = 2.0 * TD * jnp.exp2((scale_ids - (NS - 1)).astype(jnp.float32) / 4.0)
    width = scale_width[:, None, None]
    offset = lag[None, :, None] - within[None, None, :]
    scaled_offset = offset.astype(jnp.float32) / width
    amplitude = math.pi ** (-0.25) * lax.rsqrt(width) * jnp.exp(-0.5 * scaled_offset * scaled_offset)
    inside = jnp.abs(offset) < (reaches * BLK)[:, None, None]
    lag_phase = 6.0 * (lag.astype(jnp.float32)[None, :] / scale_width[:, None])
    time_phase = 6.0 * (within.astype(jnp.float32)[None, :] / scale_width[:, None])
    lag_cos = jnp.cos(lag_phase)[:, :, None]
    lag_sin = jnp.sin(lag_phase)[:, :, None]
    time_cos = jnp.cos(time_phase)[:, None, :]
    time_sin = jnp.sin(time_phase)[:, None, :]
    cos_part = lag_cos * time_cos + lag_sin * time_sin
    sin_part = lag_sin * time_cos - lag_cos * time_sin
    real_part = jnp.where(inside, amplitude * cos_part, 0.0).astype(jnp.bfloat16)
    imag_part = jnp.where(inside, amplitude * sin_part, 0.0).astype(jnp.bfloat16)
    return jnp.stack([real_part, imag_part], axis=1)


def band_coefficients(extended, scale_ids, reaches, offsets):
    channels = extended.shape[0]
    table = kernel_table(scale_ids, reaches, offsets)
    coefficients = jnp.einsum("cm,qrmt->qrct", extended, table, preferred_element_type=jnp.float32)
    scale_count = scale_ids.shape[0]
    return coefficients.astype(jnp.bfloat16).reshape(scale_count, 2 * channels, BLK)


def pair_sums(coefficients, first_flat, second_flat):
    scale_count = coefficients.shape[0]
    channels = coefficients.shape[1] // 2
    time_span = coefficients.shape[2]
    chan_iota = jnp.arange(channels, dtype=jnp.int32)
    both = jnp.concatenate([first_flat, second_flat])
    pick = (both[:, None] == chan_iota[None, :]).astype(jnp.bfloat16)
    parts = coefficients.reshape(scale_count, 2, channels, time_span)
    picked = jnp.einsum("pc,qrct->qrpt", pick, parts, preferred_element_type=jnp.bfloat16)
    pairs = first_flat.shape[0]
    first_real = picked[:, 0, :pairs]
    first_imag = picked[:, 1, :pairs]
    second_real = picked[:, 0, pairs:]
    second_imag = picked[:, 1, pairs:]

    def time_sum(left, right):
        return jnp.einsum("qpt,qpt->qp", left, right, preferred_element_type=jnp.float32)

    cross_real = time_sum(first_real, second_real) + time_sum(first_imag, second_imag)
    cross_imag = time_sum(first_imag, second_real) - time_sum(first_real, second_imag)
    power_first = time_sum(first_real, first_real) + time_sum(first_imag, first_imag)
    power_second = time_sum(second_real, second_real) + time_sum(second_imag, second_imag)
    return jnp.stack([cross_real, cross_imag, power_first, power_second], axis=1)


def shards(signal, support, pair_first, pair_second, pair_count):
    groups = lax.axis_size("chan")
    cluster_number = lax.axis_index("chan")
    time_index = lax.axis_index("tm")
    time_devices = lax.axis_size("tm")
    time_span = signal.shape[1]
    ntime = time_span * time_devices
    rounded = signal.astype(jnp.bfloat16)
    gathered = lax.all_gather(rounded, "chan", axis=0, tiled=True)
    near = jnp.concatenate(
        [from_behind(gathered, "tm", 1), gathered, from_behind(gathered, "tm", -1)], axis=1
    )
    wide = jnp.concatenate([from_behind(near, "tm", 3), near, from_behind(near, "tm", -3)], axis=1)
    per_group = NS // groups
    band = NS // 4
    narrow_count = (NS - band) // groups
    wide_count = band // groups
    narrow_ids = cluster_number * narrow_count + jnp.arange(narrow_count, dtype=jnp.int32)
    wide_ids = NS - band + cluster_number * wide_count + jnp.arange(wide_count, dtype=jnp.int32)
    narrow_coefficients = band_coefficients(near, narrow_ids, support[narrow_ids], 1)
    wide_coefficients = band_coefficients(wide, wide_ids, support[wide_ids], 4)
    owner_devices, slots_total = pair_first.shape
    slots_local = slots_total // time_devices

    def by_block(pairs):
        return pairs.reshape(owner_devices, time_devices, slots_local).transpose(1, 0, 2).reshape(-1)

    first_flat = by_block(pair_first)
    second_flat = by_block(pair_second)
    sums = jnp.concatenate(
        [
            pair_sums(narrow_coefficients, first_flat, second_flat),
            pair_sums(wide_coefficients, first_flat, second_flat),
        ],
        axis=0,
    )
    values = sums.shape[1]
    destinations = time_devices * groups
    partial_value = sums.reshape(per_group * values, -1).T.reshape(destinations, -1)
    exchanged = lax.all_to_all(partial_value, ("tm", "chan"), 0, 0, tiled=True)
    summed = jnp.sum(exchanged.reshape(time_devices, groups, -1), axis=0)
    owned = summed.reshape(groups, slots_local, per_group, values).transpose(0, 2, 3, 1) / ntime
    owned = owned.reshape(groups, per_group, values, slots_local)
    owned = jnp.concatenate(
        [
            owned[:, :narrow_count].reshape(groups * narrow_count, values, slots_local),
            owned[:, narrow_count:].reshape(groups * wide_count, values, slots_local),
        ],
        axis=0,
    )
    slot_index = time_index * slots_local + jnp.arange(slots_local, dtype=jnp.int32)
    alive_mask = slot_index < pair_count[cluster_number]
    cross_real = owned[:, 0, :].T
    cross_imag = owned[:, 1, :].T
    first_power = owned[:, 2, :].T
    second_power = owned[:, 3, :].T
    coherence = (cross_real * cross_real + cross_imag * cross_imag) / (
        (first_power + power_floor) * (second_power + power_floor)
    )
    coherence = jnp.where(alive_mask[:, None], coherence, 0.0)[None]
    cross = jnp.stack([cross_real, cross_imag], axis=1)
    cross = jnp.where(alive_mask[:, None, None], cross, 0.0)[None]
    return (cross, coherence.astype(jnp.float32))


def solution(mesh):
    in_specs = (P("chan", "tm"), P(), P(), P(), P())
    out_specs = (P("chan", "tm", None, None), P("chan", "tm", None))
    return jax.shard_map(shards, mesh=mesh, in_specs=in_specs, out_specs=out_specs, check_vma=False)
```

```python
import math

import jax
import jax.numpy as jnp
import numpy as np
from jax import lax
from jax.sharding import PartitionSpec as P

NS = 32
BLK = 128
TD = 128


power_floor = 1e-06


def from_behind(array, axis, by):
    peers = lax.axis_size(axis)
    return lax.ppermute(array, axis, [(i, (i + by) % peers) for i in range(peers)])


def kernel_table(scale_ids, reaches, offsets):
    taps = (2 * offsets + 1) * BLK
    lag = jnp.arange(taps, dtype=jnp.int32) - offsets * BLK
    within = jnp.arange(BLK, dtype=jnp.int32)
    scale_width = 2.0 * TD * jnp.exp2((scale_ids - (NS - 1)).astype(jnp.float32) / 4.0)
    width = scale_width[:, None, None]
    offset = lag[None, :, None] - within[None, None, :]
    scaled_offset = offset.astype(jnp.float32) / width
    amplitude = math.pi ** (-0.25) * lax.rsqrt(width) * jnp.exp(-0.5 * scaled_offset * scaled_offset)
    inside = jnp.abs(offset) < (reaches * BLK)[:, None, None]
    lag_phase = 6.0 * (lag.astype(jnp.float32)[None, :] / scale_width[:, None])
    time_phase = 6.0 * (within.astype(jnp.float32)[None, :] / scale_width[:, None])
    lag_cos = jnp.cos(lag_phase)[:, :, None]
    lag_sin = jnp.sin(lag_phase)[:, :, None]
    time_cos = jnp.cos(time_phase)[:, None, :]
    time_sin = jnp.sin(time_phase)[:, None, :]
    cos_part = lag_cos * time_cos + lag_sin * time_sin
    sin_part = lag_sin * time_cos - lag_cos * time_sin
    real_part = jnp.where(inside, amplitude * cos_part, 0.0).astype(jnp.bfloat16)
    imag_part = jnp.where(inside, amplitude * sin_part, 0.0).astype(jnp.bfloat16)
    return jnp.stack([real_part, imag_part], axis=1)


def band_coefficients(extended, scale_ids, reaches, offsets):
    channels = extended.shape[0]
    table = kernel_table(scale_ids, reaches, offsets)
    coefficients = jnp.einsum("cm,qrmt->qrct", extended, table, preferred_element_type=jnp.float32)
    scale_count = scale_ids.shape[0]
    return coefficients.astype(jnp.bfloat16).reshape(scale_count, 2 * channels, BLK)


def pair_sums(coefficients, first_flat, second_flat):
    scale_count = coefficients.shape[0]
    channels = coefficients.shape[1] // 2
    time_span = coefficients.shape[2]
    chan_iota = jnp.arange(channels, dtype=jnp.int32)
    both = jnp.concatenate([first_flat, second_flat])
    pick = (both[:, None] == chan_iota[None, :]).astype(jnp.bfloat16)
    parts = coefficients.reshape(scale_count, 2, channels, time_span)
    picked = jnp.einsum("pc,qrct->qrpt", pick, parts, preferred_element_type=jnp.bfloat16)
    pairs = first_flat.shape[0]
    first_real = picked[:, 0, :pairs]
    first_imag = picked[:, 1, :pairs]
    second_real = picked[:, 0, pairs:]
    second_imag = picked[:, 1, pairs:]

    def time_sum(left, right):
        return jnp.einsum("qpt,qpt->qp", left, right, preferred_element_type=jnp.float32)

    cross_real = time_sum(first_real, second_real) + time_sum(first_imag, second_imag)
    cross_imag = time_sum(first_imag, second_real) - time_sum(first_real, second_imag)
    power_first = time_sum(first_real, first_real) + time_sum(first_imag, first_imag)
    power_second = time_sum(second_real, second_real) + time_sum(second_imag, second_imag)
    return jnp.stack([cross_real, cross_imag, power_first, power_second], axis=1)


def shards(signal, support, pair_first, pair_second, pair_count):
    groups = lax.axis_size("chan")
    cluster_number = lax.axis_index("chan")
    time_index = lax.axis_index("tm")
    time_devices = lax.axis_size("tm")
    time_span = signal.shape[1]
    ntime = time_span * time_devices
    rounded = signal.astype(jnp.bfloat16)
    triple = jnp.concatenate(
        [from_behind(rounded, "tm", 1), rounded, from_behind(rounded, "tm", -1)], axis=1
    )
    near = lax.all_gather(triple, "chan", axis=0, tiled=True)
    wide = jnp.concatenate([from_behind(near, "tm", 3), near, from_behind(near, "tm", -3)], axis=1)
    per_group = NS // groups
    band = NS // 4
    narrow_count = (NS - band) // groups
    wide_count = band // groups
    narrow_ids = cluster_number * narrow_count + jnp.arange(narrow_count, dtype=jnp.int32)
    wide_ids = NS - band + cluster_number * wide_count + jnp.arange(wide_count, dtype=jnp.int32)
    narrow_coefficients = band_coefficients(near, narrow_ids, support[narrow_ids], 1)
    wide_coefficients = band_coefficients(wide, wide_ids, support[wide_ids], 4)
    owner_devices, slots_total = pair_first.shape
    slots_local = slots_total // time_devices

    def by_block(pairs):
        return pairs.reshape(owner_devices, time_devices, slots_local).transpose(1, 0, 2).reshape(-1)

    first_flat = by_block(pair_first)
    second_flat = by_block(pair_second)
    sums = jnp.concatenate(
        [
            pair_sums(narrow_coefficients, first_flat, second_flat),
            pair_sums(wide_coefficients, first_flat, second_flat),
        ],
        axis=0,
    )
    values = sums.shape[1]
    destinations = time_devices * groups
    partial_value = sums.reshape(per_group * values, -1).T.reshape(destinations, -1)
    exchanged = lax.all_to_all(partial_value, ("tm", "chan"), 0, 0, tiled=True)
    summed = jnp.sum(exchanged.reshape(time_devices, groups, -1), axis=0)
    owned = summed.reshape(groups, slots_local, per_group, values).transpose(0, 2, 3, 1) / ntime
    owned = owned.reshape(groups, per_group, values, slots_local)
    owned = jnp.concatenate(
        [
            owned[:, :narrow_count].reshape(groups * narrow_count, values, slots_local),
            owned[:, narrow_count:].reshape(groups * wide_count, values, slots_local),
        ],
        axis=0,
    )
    slot_index = time_index * slots_local + jnp.arange(slots_local, dtype=jnp.int32)
    alive_mask = slot_index < pair_count[cluster_number]
    cross_real = owned[:, 0, :].T
    cross_imag = owned[:, 1, :].T
    first_power = owned[:, 2, :].T
    second_power = owned[:, 3, :].T
    coherence = (cross_real * cross_real + cross_imag * cross_imag) / (
        (first_power + power_floor) * (second_power + power_floor)
    )
    coherence = jnp.where(alive_mask[:, None], coherence, 0.0)[None]
    cross = jnp.stack([cross_real, cross_imag], axis=1)
    cross = jnp.where(alive_mask[:, None, None], cross, 0.0)[None]
    return (cross, coherence.astype(jnp.float32))


def solution(mesh):
    in_specs = (P("chan", "tm"), P(), P(), P(), P())
    out_specs = (P("chan", "tm", None, None), P("chan", "tm", None))
    return jax.shard_map(shards, mesh=mesh, in_specs=in_specs, out_specs=out_specs, check_vma=False)
```

```python
import math

import jax
import jax.numpy as jnp
import numpy as np
from jax import lax
from jax.sharding import PartitionSpec as P

NS = 32
BLK = 128
TD = 128


power_floor = 1e-06


def from_behind(array, axis, by):
    peers = lax.axis_size(axis)
    return lax.ppermute(array, axis, [(i, (i + by) % peers) for i in range(peers)])


def kernel_table(scale_ids, reaches, offsets):
    taps = (2 * offsets + 1) * BLK
    lag = jnp.arange(taps, dtype=jnp.int32) - offsets * BLK
    within = jnp.arange(BLK, dtype=jnp.int32)
    scale_width = 2.0 * TD * jnp.exp2((scale_ids - (NS - 1)).astype(jnp.float32) / 4.0)
    width = scale_width[:, None, None]
    offset = lag[None, :, None] - within[None, None, :]
    scaled_offset = offset.astype(jnp.float32) / width
    amplitude = math.pi ** (-0.25) * lax.rsqrt(width) * jnp.exp(-0.5 * scaled_offset * scaled_offset)
    inside = jnp.abs(offset) < (reaches * BLK)[:, None, None]
    lag_phase = 6.0 * (lag.astype(jnp.float32)[None, :] / scale_width[:, None])
    time_phase = 6.0 * (within.astype(jnp.float32)[None, :] / scale_width[:, None])
    lag_cos = jnp.cos(lag_phase)[:, :, None]
    lag_sin = jnp.sin(lag_phase)[:, :, None]
    time_cos = jnp.cos(time_phase)[:, None, :]
    time_sin = jnp.sin(time_phase)[:, None, :]
    cos_part = lag_cos * time_cos + lag_sin * time_sin
    sin_part = lag_sin * time_cos - lag_cos * time_sin
    real_part = jnp.where(inside, amplitude * cos_part, 0.0).astype(jnp.bfloat16)
    imag_part = jnp.where(inside, amplitude * sin_part, 0.0).astype(jnp.bfloat16)
    return jnp.stack([real_part, imag_part], axis=1)


def band_coefficients(extended, scale_ids, reaches, offsets):
    channels = extended.shape[0]
    table = kernel_table(scale_ids, reaches, offsets)
    coefficients = jnp.einsum("cm,qrmt->qrct", extended, table, preferred_element_type=jnp.float32)
    scale_count = scale_ids.shape[0]
    return coefficients.astype(jnp.bfloat16).reshape(scale_count, 2 * channels, BLK)


def pair_sums(coefficients, first_flat, second_flat):
    scale_count = coefficients.shape[0]
    channels = coefficients.shape[1] // 2
    time_span = coefficients.shape[2]
    chan_iota = jnp.arange(channels, dtype=jnp.int32)
    both = jnp.concatenate([first_flat, second_flat])
    pick = (both[:, None] == chan_iota[None, :]).astype(jnp.bfloat16)
    parts = coefficients.reshape(scale_count, 2, channels, time_span)
    picked = jnp.einsum("pc,qrct->qrpt", pick, parts, preferred_element_type=jnp.bfloat16)
    pairs = first_flat.shape[0]
    first_real = picked[:, 0, :pairs]
    first_imag = picked[:, 1, :pairs]
    second_real = picked[:, 0, pairs:]
    second_imag = picked[:, 1, pairs:]

    def time_sum(left, right):
        return jnp.einsum("qpt,qpt->qp", left, right, preferred_element_type=jnp.float32)

    cross_real = time_sum(first_real, second_real) + time_sum(first_imag, second_imag)
    cross_imag = time_sum(first_imag, second_real) - time_sum(first_real, second_imag)
    power = jnp.einsum("qrct,qrct->qc", parts, parts, preferred_element_type=jnp.float32)
    owner_power = jnp.einsum(
        "pc,qc->qp", pick.astype(jnp.float32), power, precision=lax.Precision.HIGHEST
    )
    power_first = owner_power[:, :pairs]
    power_second = owner_power[:, pairs:]
    return jnp.stack([cross_real, cross_imag, power_first, power_second], axis=1)


def shards(signal, support, pair_first, pair_second, pair_count):
    groups = lax.axis_size("chan")
    cluster_number = lax.axis_index("chan")
    time_index = lax.axis_index("tm")
    time_devices = lax.axis_size("tm")
    time_span = signal.shape[1]
    ntime = time_span * time_devices
    rounded = signal.astype(jnp.bfloat16)
    gathered = lax.all_gather(rounded, "chan", axis=0, tiled=True)
    near = jnp.concatenate(
        [from_behind(gathered, "tm", 1), gathered, from_behind(gathered, "tm", -1)], axis=1
    )
    wide = jnp.concatenate([from_behind(near, "tm", 3), near, from_behind(near, "tm", -3)], axis=1)
    per_group = NS // groups
    band = NS // 4
    narrow_count = (NS - band) // groups
    wide_count = band // groups
    narrow_ids = cluster_number * narrow_count + jnp.arange(narrow_count, dtype=jnp.int32)
    wide_ids = NS - band + cluster_number * wide_count + jnp.arange(wide_count, dtype=jnp.int32)
    narrow_coefficients = band_coefficients(near, narrow_ids, support[narrow_ids], 1)
    wide_coefficients = band_coefficients(wide, wide_ids, support[wide_ids], 4)
    owner_devices, slots_total = pair_first.shape
    slots_local = slots_total // time_devices

    def by_block(pairs):
        return pairs.reshape(owner_devices, time_devices, slots_local).transpose(1, 0, 2).reshape(-1)

    first_flat = by_block(pair_first)
    second_flat = by_block(pair_second)
    sums = jnp.concatenate(
        [
            pair_sums(narrow_coefficients, first_flat, second_flat),
            pair_sums(wide_coefficients, first_flat, second_flat),
        ],
        axis=0,
    )
    values = sums.shape[1]
    destinations = time_devices * groups
    partial_value = sums.reshape(per_group * values, -1).T.reshape(destinations, -1)
    exchanged = lax.all_to_all(partial_value, ("tm", "chan"), 0, 0, tiled=True)
    summed = jnp.sum(exchanged.reshape(time_devices, groups, -1), axis=0)
    owned = summed.reshape(groups, slots_local, per_group, values).transpose(0, 2, 3, 1) / ntime
    owned = owned.reshape(groups, per_group, values, slots_local)
    owned = jnp.concatenate(
        [
            owned[:, :narrow_count].reshape(groups * narrow_count, values, slots_local),
            owned[:, narrow_count:].reshape(groups * wide_count, values, slots_local),
        ],
        axis=0,
    )
    slot_index = time_index * slots_local + jnp.arange(slots_local, dtype=jnp.int32)
    alive_mask = slot_index < pair_count[cluster_number]
    cross_real = owned[:, 0, :].T
    cross_imag = owned[:, 1, :].T
    first_power = owned[:, 2, :].T
    second_power = owned[:, 3, :].T
    coherence = (cross_real * cross_real + cross_imag * cross_imag) / (
        (first_power + power_floor) * (second_power + power_floor)
    )
    coherence = jnp.where(alive_mask[:, None], coherence, 0.0)[None]
    cross = jnp.stack([cross_real, cross_imag], axis=1)
    cross = jnp.where(alive_mask[:, None, None], cross, 0.0)[None]
    return (cross, coherence.astype(jnp.float32))


def solution(mesh):
    in_specs = (P("chan", "tm"), P(), P(), P(), P())
    out_specs = (P("chan", "tm", None, None), P("chan", "tm", None))
    return jax.shard_map(shards, mesh=mesh, in_specs=in_specs, out_specs=out_specs, check_vma=False)
```

```python
import math

import jax
import jax.numpy as jnp
import numpy as np
from jax import lax
from jax.sharding import PartitionSpec as P

NS = 32
BLK = 128
TD = 128


power_floor = 1e-06


def from_behind(array, axis, by):
    peers = lax.axis_size(axis)
    return lax.ppermute(array, axis, [(i, (i + by) % peers) for i in range(peers)])


def kernel_table(scale_ids, reaches, offsets):
    taps = (2 * offsets + 1) * BLK
    lag = jnp.arange(taps, dtype=jnp.int32) - offsets * BLK
    within = jnp.arange(BLK, dtype=jnp.int32)
    scale_width = 2.0 * TD * jnp.exp2((scale_ids - (NS - 1)).astype(jnp.float32) / 4.0)
    width = scale_width[:, None, None]
    offset = lag[None, :, None] - within[None, None, :]
    scaled_offset = offset.astype(jnp.float32) / width
    amplitude = math.pi ** (-0.25) * lax.rsqrt(width) * jnp.exp(-0.5 * scaled_offset * scaled_offset)
    inside = jnp.abs(offset) < (reaches * BLK)[:, None, None]
    lag_phase = 6.0 * (lag.astype(jnp.float32)[None, :] / scale_width[:, None])
    time_phase = 6.0 * (within.astype(jnp.float32)[None, :] / scale_width[:, None])
    lag_cos = jnp.cos(lag_phase)[:, :, None]
    lag_sin = jnp.sin(lag_phase)[:, :, None]
    time_cos = jnp.cos(time_phase)[:, None, :]
    time_sin = jnp.sin(time_phase)[:, None, :]
    cos_part = lag_cos * time_cos + lag_sin * time_sin
    sin_part = lag_sin * time_cos - lag_cos * time_sin
    real_part = jnp.where(inside, amplitude * cos_part, 0.0).astype(jnp.bfloat16)
    imag_part = jnp.where(inside, amplitude * sin_part, 0.0).astype(jnp.bfloat16)
    return jnp.stack([real_part, imag_part], axis=1)


def band_coefficients(extended, scale_ids, reaches, offsets):
    channels = extended.shape[0]
    table = kernel_table(scale_ids, reaches, offsets)
    coefficients = jnp.einsum("cm,qrmt->qrct", extended, table, preferred_element_type=jnp.float32)
    scale_count = scale_ids.shape[0]
    return coefficients.astype(jnp.bfloat16).reshape(scale_count, 2 * channels, BLK)


def pair_sums(coefficients, first_flat, second_flat):
    scale_count = coefficients.shape[0]
    channels = coefficients.shape[1] // 2
    time_span = coefficients.shape[2]
    chan_iota = jnp.arange(channels, dtype=jnp.int32)
    both = jnp.concatenate([first_flat, second_flat])
    pick = (both[:, None] == chan_iota[None, :]).astype(jnp.bfloat16)
    parts = coefficients.reshape(scale_count, 2, channels, time_span)
    picked = jnp.einsum("pc,qrct->qrpt", pick, parts, preferred_element_type=jnp.bfloat16)
    pairs = first_flat.shape[0]
    first_real = picked[:, 0, :pairs]
    first_imag = picked[:, 1, :pairs]
    second_real = picked[:, 0, pairs:]
    second_imag = picked[:, 1, pairs:]

    def time_sum(left, right):
        return jnp.einsum("qpt,qpt->qp", left, right, preferred_element_type=jnp.float32)

    cross_real = time_sum(first_real, second_real) + time_sum(first_imag, second_imag)
    cross_imag = time_sum(first_imag, second_real) - time_sum(first_real, second_imag)
    power = jnp.einsum("qrct,qrct->qc", parts, parts, preferred_element_type=jnp.float32)
    high = power.astype(jnp.bfloat16)
    rest = power - high.astype(jnp.float32)
    middle = rest.astype(jnp.bfloat16)
    low = (rest - middle.astype(jnp.float32)).astype(jnp.bfloat16)
    pieces = jnp.stack([high, middle, low])
    picked_power = jnp.einsum("pc,kqc->kqp", pick, pieces, preferred_element_type=jnp.float32)
    owner_power = (picked_power[0] + picked_power[1]) + picked_power[2]
    power_first = owner_power[:, :pairs]
    power_second = owner_power[:, pairs:]
    return jnp.stack([cross_real, cross_imag, power_first, power_second], axis=1)


def shards(signal, support, pair_first, pair_second, pair_count):
    groups = lax.axis_size("chan")
    cluster_number = lax.axis_index("chan")
    time_index = lax.axis_index("tm")
    time_devices = lax.axis_size("tm")
    time_span = signal.shape[1]
    ntime = time_span * time_devices
    rounded = signal.astype(jnp.bfloat16)
    gathered = lax.all_gather(rounded, "chan", axis=0, tiled=True)
    near = jnp.concatenate(
        [from_behind(gathered, "tm", 1), gathered, from_behind(gathered, "tm", -1)], axis=1
    )
    wide = jnp.concatenate([from_behind(near, "tm", 3), near, from_behind(near, "tm", -3)], axis=1)
    per_group = NS // groups
    band = NS // 4
    narrow_count = (NS - band) // groups
    wide_count = band // groups
    narrow_ids = cluster_number * narrow_count + jnp.arange(narrow_count, dtype=jnp.int32)
    wide_ids = NS - band + cluster_number * wide_count + jnp.arange(wide_count, dtype=jnp.int32)
    narrow_coefficients = band_coefficients(near, narrow_ids, support[narrow_ids], 1)
    wide_coefficients = band_coefficients(wide, wide_ids, support[wide_ids], 4)
    owner_devices, slots_total = pair_first.shape
    slots_local = slots_total // time_devices

    def by_block(pairs):
        return pairs.reshape(owner_devices, time_devices, slots_local).transpose(1, 0, 2).reshape(-1)

    first_flat = by_block(pair_first)
    second_flat = by_block(pair_second)
    sums = jnp.concatenate(
        [
            pair_sums(narrow_coefficients, first_flat, second_flat),
            pair_sums(wide_coefficients, first_flat, second_flat),
        ],
        axis=0,
    )
    values = sums.shape[1]
    destinations = time_devices * groups
    partial_value = sums.reshape(per_group * values, -1).T.reshape(destinations, -1)
    exchanged = lax.all_to_all(partial_value, ("tm", "chan"), 0, 0, tiled=True)
    summed = jnp.sum(exchanged.reshape(time_devices, groups, -1), axis=0)
    owned = summed.reshape(groups, slots_local, per_group, values).transpose(0, 2, 3, 1) / ntime
    owned = owned.reshape(groups, per_group, values, slots_local)
    owned = jnp.concatenate(
        [
            owned[:, :narrow_count].reshape(groups * narrow_count, values, slots_local),
            owned[:, narrow_count:].reshape(groups * wide_count, values, slots_local),
        ],
        axis=0,
    )
    slot_index = time_index * slots_local + jnp.arange(slots_local, dtype=jnp.int32)
    alive_mask = slot_index < pair_count[cluster_number]
    cross_real = owned[:, 0, :].T
    cross_imag = owned[:, 1, :].T
    first_power = owned[:, 2, :].T
    second_power = owned[:, 3, :].T
    coherence = (cross_real * cross_real + cross_imag * cross_imag) / (
        (first_power + power_floor) * (second_power + power_floor)
    )
    coherence = jnp.where(alive_mask[:, None], coherence, 0.0)[None]
    cross = jnp.stack([cross_real, cross_imag], axis=1)
    cross = jnp.where(alive_mask[:, None, None], cross, 0.0)[None]
    return (cross, coherence.astype(jnp.float32))


def solution(mesh):
    in_specs = (P("chan", "tm"), P(), P(), P(), P())
    out_specs = (P("chan", "tm", None, None), P("chan", "tm", None))
    return jax.shard_map(shards, mesh=mesh, in_specs=in_specs, out_specs=out_specs, check_vma=False)
```

```python
import math

import jax
import jax.numpy as jnp
import numpy as np
from jax import lax
from jax.sharding import PartitionSpec as P

NS = 32
BLK = 128
TD = 128


power_floor = 1e-06


def from_behind(array, axis, by):
    peers = lax.axis_size(axis)
    return lax.ppermute(array, axis, [(i, (i + by) % peers) for i in range(peers)])


def kernel_table(scale_ids, reaches, offsets):
    taps = (2 * offsets + 1) * BLK
    lag = jnp.arange(taps, dtype=jnp.int32) - offsets * BLK
    within = jnp.arange(BLK, dtype=jnp.int32)
    scale_width = 2.0 * TD * jnp.exp2((scale_ids - (NS - 1)).astype(jnp.float32) / 4.0)
    width = scale_width[:, None, None]
    offset = lag[None, :, None] - within[None, None, :]
    scaled_offset = offset.astype(jnp.float32) / width
    amplitude = math.pi ** (-0.25) * lax.rsqrt(width) * jnp.exp(-0.5 * scaled_offset * scaled_offset)
    inside = jnp.abs(offset) < (reaches * BLK)[:, None, None]
    lag_phase = 6.0 * (lag.astype(jnp.float32)[None, :] / scale_width[:, None])
    time_phase = 6.0 * (within.astype(jnp.float32)[None, :] / scale_width[:, None])
    lag_cos = jnp.cos(lag_phase)[:, :, None]
    lag_sin = jnp.sin(lag_phase)[:, :, None]
    time_cos = jnp.cos(time_phase)[:, None, :]
    time_sin = jnp.sin(time_phase)[:, None, :]
    cos_part = lag_cos * time_cos + lag_sin * time_sin
    sin_part = lag_sin * time_cos - lag_cos * time_sin
    real_part = jnp.where(inside, amplitude * cos_part, 0.0).astype(jnp.bfloat16)
    imag_part = jnp.where(inside, amplitude * sin_part, 0.0).astype(jnp.bfloat16)
    return jnp.stack([real_part, imag_part], axis=1)


def band_coefficients(extended, scale_ids, reaches, offsets):
    channels = extended.shape[0]
    table = kernel_table(scale_ids, reaches, offsets)
    coefficients = jnp.einsum("cm,qrmt->qrct", extended, table, preferred_element_type=jnp.float32)
    scale_count = scale_ids.shape[0]
    return coefficients.astype(jnp.bfloat16).reshape(scale_count, 2 * channels, BLK)


def pair_sums(coefficients, first_flat, second_flat):
    scale_count = coefficients.shape[0]
    channels = coefficients.shape[1] // 2
    time_span = coefficients.shape[2]
    chan_iota = jnp.arange(channels, dtype=jnp.int32)
    both = jnp.concatenate([first_flat, second_flat])
    pick = (both[:, None] == chan_iota[None, :]).astype(jnp.bfloat16)
    parts = coefficients.reshape(scale_count, 2, channels, time_span)
    picked = jnp.einsum("pc,qrct->qrpt", pick, parts, preferred_element_type=jnp.bfloat16)
    pairs = first_flat.shape[0]
    first_real = picked[:, 0, :pairs]
    first_imag = picked[:, 1, :pairs]
    second_real = picked[:, 0, pairs:]
    second_imag = picked[:, 1, pairs:]

    def time_sum(left, right):
        return jnp.einsum("qpt,qpt->qp", left, right, preferred_element_type=jnp.float32)

    cross_real = time_sum(first_real, second_real) + time_sum(first_imag, second_imag)
    cross_imag = time_sum(first_imag, second_real) - time_sum(first_real, second_imag)
    power = jnp.einsum("qrct,qrct->qc", parts, parts, preferred_element_type=jnp.float32)
    high = lax.reduce_precision(power, exponent_bits=8, mantissa_bits=7)
    rest = power - high
    middle = lax.reduce_precision(rest, exponent_bits=8, mantissa_bits=7)
    low = rest - middle
    pieces = jnp.stack([high, middle, low]).astype(jnp.bfloat16)
    picked_power = jnp.einsum("pc,kqc->kqp", pick, pieces, preferred_element_type=jnp.float32)
    owner_power = (picked_power[0] + picked_power[1]) + picked_power[2]
    power_first = owner_power[:, :pairs]
    power_second = owner_power[:, pairs:]
    return jnp.stack([cross_real, cross_imag, power_first, power_second], axis=1)


def shards(signal, support, pair_first, pair_second, pair_count):
    groups = lax.axis_size("chan")
    cluster_number = lax.axis_index("chan")
    time_index = lax.axis_index("tm")
    time_devices = lax.axis_size("tm")
    time_span = signal.shape[1]
    ntime = time_span * time_devices
    rounded = signal.astype(jnp.bfloat16)
    gathered = lax.all_gather(rounded, "chan", axis=0, tiled=True)
    near = jnp.concatenate(
        [from_behind(gathered, "tm", 1), gathered, from_behind(gathered, "tm", -1)], axis=1
    )
    wide = jnp.concatenate([from_behind(near, "tm", 3), near, from_behind(near, "tm", -3)], axis=1)
    per_group = NS // groups
    band = NS // 4
    narrow_count = (NS - band) // groups
    wide_count = band // groups
    narrow_ids = cluster_number * narrow_count + jnp.arange(narrow_count, dtype=jnp.int32)
    wide_ids = NS - band + cluster_number * wide_count + jnp.arange(wide_count, dtype=jnp.int32)
    narrow_coefficients = band_coefficients(near, narrow_ids, support[narrow_ids], 1)
    wide_coefficients = band_coefficients(wide, wide_ids, support[wide_ids], 4)
    owner_devices, slots_total = pair_first.shape
    slots_local = slots_total // time_devices

    def by_block(pairs):
        return pairs.reshape(owner_devices, time_devices, slots_local).transpose(1, 0, 2).reshape(-1)

    first_flat = by_block(pair_first)
    second_flat = by_block(pair_second)
    sums = jnp.concatenate(
        [
            pair_sums(narrow_coefficients, first_flat, second_flat),
            pair_sums(wide_coefficients, first_flat, second_flat),
        ],
        axis=0,
    )
    values = sums.shape[1]
    destinations = time_devices * groups
    partial_value = sums.reshape(per_group * values, -1).T.reshape(destinations, -1)
    exchanged = lax.all_to_all(partial_value, ("tm", "chan"), 0, 0, tiled=True)
    summed = jnp.sum(exchanged.reshape(time_devices, groups, -1), axis=0)
    owned = summed.reshape(groups, slots_local, per_group, values).transpose(0, 2, 3, 1) / ntime
    owned = owned.reshape(groups, per_group, values, slots_local)
    owned = jnp.concatenate(
        [
            owned[:, :narrow_count].reshape(groups * narrow_count, values, slots_local),
            owned[:, narrow_count:].reshape(groups * wide_count, values, slots_local),
        ],
        axis=0,
    )
    slot_index = time_index * slots_local + jnp.arange(slots_local, dtype=jnp.int32)
    alive_mask = slot_index < pair_count[cluster_number]
    cross_real = owned[:, 0, :].T
    cross_imag = owned[:, 1, :].T
    first_power = owned[:, 2, :].T
    second_power = owned[:, 3, :].T
    coherence = (cross_real * cross_real + cross_imag * cross_imag) / (
        (first_power + power_floor) * (second_power + power_floor)
    )
    coherence = jnp.where(alive_mask[:, None], coherence, 0.0)[None]
    cross = jnp.stack([cross_real, cross_imag], axis=1)
    cross = jnp.where(alive_mask[:, None, None], cross, 0.0)[None]
    return (cross, coherence.astype(jnp.float32))


def solution(mesh):
    in_specs = (P("chan", "tm"), P(), P(), P(), P())
    out_specs = (P("chan", "tm", None, None), P("chan", "tm", None))
    return jax.shard_map(shards, mesh=mesh, in_specs=in_specs, out_specs=out_specs, check_vma=False)
```

```python
import math

import jax
import jax.numpy as jnp
import numpy as np
from jax import lax
from jax.sharding import PartitionSpec as P

NS = 32
BLK = 128
TD = 128


power_floor = 1e-06


def from_behind(array, axis, by):
    peers = lax.axis_size(axis)
    return lax.ppermute(array, axis, [(i, (i + by) % peers) for i in range(peers)])


def kernel_table(scale_ids, reaches, offsets):
    taps = (2 * offsets + 1) * BLK
    lag = jnp.arange(taps, dtype=jnp.int32) - offsets * BLK
    within = jnp.arange(BLK, dtype=jnp.int32)
    scale_width = 2.0 * TD * jnp.exp2((scale_ids - (NS - 1)).astype(jnp.float32) / 4.0)
    width = scale_width[:, None, None]
    offset = lag[None, :, None] - within[None, None, :]
    scaled_offset = offset.astype(jnp.float32) / width
    amplitude = math.pi ** (-0.25) * lax.rsqrt(width) * jnp.exp(-0.5 * scaled_offset * scaled_offset)
    inside = jnp.abs(offset) < (reaches * BLK)[:, None, None]
    lag_phase = 6.0 * (lag.astype(jnp.float32)[None, :] / scale_width[:, None])
    time_phase = 6.0 * (within.astype(jnp.float32)[None, :] / scale_width[:, None])
    lag_cos = jnp.cos(lag_phase)[:, :, None]
    lag_sin = jnp.sin(lag_phase)[:, :, None]
    time_cos = jnp.cos(time_phase)[:, None, :]
    time_sin = jnp.sin(time_phase)[:, None, :]
    cos_part = lag_cos * time_cos + lag_sin * time_sin
    sin_part = lag_sin * time_cos - lag_cos * time_sin
    real_part = jnp.where(inside, amplitude * cos_part, 0.0).astype(jnp.bfloat16)
    imag_part = jnp.where(inside, amplitude * sin_part, 0.0).astype(jnp.bfloat16)
    return jnp.stack([real_part, imag_part], axis=1)


def band_coefficients(extended, scale_ids, reaches, offsets):
    channels = extended.shape[0]
    table = kernel_table(scale_ids, reaches, offsets)
    coefficients = jnp.einsum("cm,qrmt->qrct", extended, table, preferred_element_type=jnp.float32)
    scale_count = scale_ids.shape[0]
    return coefficients.astype(jnp.bfloat16).reshape(scale_count, 2 * channels, BLK)


def pair_sums(coefficients, first_flat, second_flat):
    scale_count = coefficients.shape[0]
    channels = coefficients.shape[1] // 2
    time_span = coefficients.shape[2]
    chan_iota = jnp.arange(channels, dtype=jnp.int32)
    both = jnp.concatenate([first_flat, second_flat])
    pick = (both[:, None] == chan_iota[None, :]).astype(jnp.bfloat16)
    parts = coefficients.reshape(scale_count, 2, channels, time_span)
    picked = jnp.einsum("pc,qrct->qrpt", pick, parts, preferred_element_type=jnp.bfloat16)
    pairs = first_flat.shape[0]
    first_real = picked[:, 0, :pairs]
    first_imag = picked[:, 1, :pairs]
    second_real = picked[:, 0, pairs:]
    second_imag = picked[:, 1, pairs:]

    def time_sum(left, right):
        return jnp.einsum("qpt,qpt->qp", left, right, preferred_element_type=jnp.float32)

    cross_real = time_sum(first_real, second_real) + time_sum(first_imag, second_imag)
    cross_imag = time_sum(first_imag, second_real) - time_sum(first_real, second_imag)
    power = jnp.einsum("qrct,qrct->qc", parts, parts, preferred_element_type=jnp.float32)
    high = lax.reduce_precision(power, exponent_bits=8, mantissa_bits=7)
    rest = power - high
    middle = lax.reduce_precision(rest, exponent_bits=8, mantissa_bits=7)
    low = rest - middle
    pieces = jnp.stack([high, middle, low]).astype(jnp.bfloat16)
    picked_power = jnp.einsum("pc,kqc->kqp", pick, pieces, preferred_element_type=jnp.float32)
    owner_power = (picked_power[0] + picked_power[1]) + picked_power[2]
    power_first = owner_power[:, :pairs]
    power_second = owner_power[:, pairs:]
    return jnp.stack([cross_real, cross_imag, power_first, power_second], axis=1)


def shards(signal, support, pair_first, pair_second, pair_count):
    groups = lax.axis_size("chan")
    cluster_number = lax.axis_index("chan")
    time_index = lax.axis_index("tm")
    time_devices = lax.axis_size("tm")
    time_span = signal.shape[1]
    ntime = time_span * time_devices
    rounded = signal.astype(jnp.bfloat16)
    copies = jnp.broadcast_to(rounded[None], (groups,) + rounded.shape)
    gathered = lax.all_to_all(copies, "chan", 0, 0, tiled=True).reshape(-1, rounded.shape[1])
    near = jnp.concatenate(
        [from_behind(gathered, "tm", 1), gathered, from_behind(gathered, "tm", -1)], axis=1
    )
    wide = jnp.concatenate([from_behind(near, "tm", 3), near, from_behind(near, "tm", -3)], axis=1)
    per_group = NS // groups
    band = NS // 4
    narrow_count = (NS - band) // groups
    wide_count = band // groups
    narrow_ids = cluster_number * narrow_count + jnp.arange(narrow_count, dtype=jnp.int32)
    wide_ids = NS - band + cluster_number * wide_count + jnp.arange(wide_count, dtype=jnp.int32)
    narrow_coefficients = band_coefficients(near, narrow_ids, support[narrow_ids], 1)
    wide_coefficients = band_coefficients(wide, wide_ids, support[wide_ids], 4)
    owner_devices, slots_total = pair_first.shape
    slots_local = slots_total // time_devices

    def by_block(pairs):
        return pairs.reshape(owner_devices, time_devices, slots_local).transpose(1, 0, 2).reshape(-1)

    first_flat = by_block(pair_first)
    second_flat = by_block(pair_second)
    sums = jnp.concatenate(
        [
            pair_sums(narrow_coefficients, first_flat, second_flat),
            pair_sums(wide_coefficients, first_flat, second_flat),
        ],
        axis=0,
    )
    values = sums.shape[1]
    destinations = time_devices * groups
    partial_value = sums.reshape(per_group * values, -1).T.reshape(destinations, -1)
    exchanged = lax.all_to_all(partial_value, ("tm", "chan"), 0, 0, tiled=True)
    summed = jnp.sum(exchanged.reshape(time_devices, groups, -1), axis=0)
    owned = summed.reshape(groups, slots_local, per_group, values).transpose(0, 2, 3, 1) / ntime
    owned = owned.reshape(groups, per_group, values, slots_local)
    owned = jnp.concatenate(
        [
            owned[:, :narrow_count].reshape(groups * narrow_count, values, slots_local),
            owned[:, narrow_count:].reshape(groups * wide_count, values, slots_local),
        ],
        axis=0,
    )
    slot_index = time_index * slots_local + jnp.arange(slots_local, dtype=jnp.int32)
    alive_mask = slot_index < pair_count[cluster_number]
    cross_real = owned[:, 0, :].T
    cross_imag = owned[:, 1, :].T
    first_power = owned[:, 2, :].T
    second_power = owned[:, 3, :].T
    coherence = (cross_real * cross_real + cross_imag * cross_imag) / (
        (first_power + power_floor) * (second_power + power_floor)
    )
    coherence = jnp.where(alive_mask[:, None], coherence, 0.0)[None]
    cross = jnp.stack([cross_real, cross_imag], axis=1)
    cross = jnp.where(alive_mask[:, None, None], cross, 0.0)[None]
    return (cross, coherence.astype(jnp.float32))


def solution(mesh):
    in_specs = (P("chan", "tm"), P(), P(), P(), P())
    out_specs = (P("chan", "tm", None, None), P("chan", "tm", None))
    return jax.shard_map(shards, mesh=mesh, in_specs=in_specs, out_specs=out_specs, check_vma=False)
```

```python
import math

import jax
import jax.numpy as jnp
import numpy as np
from jax import lax
from jax.sharding import PartitionSpec as P

NS = 32
BLK = 128
TD = 128


power_floor = 1e-06


def from_behind(array, axis, by):
    peers = lax.axis_size(axis)
    return lax.ppermute(array, axis, [(i, (i + by) % peers) for i in range(peers)])


def kernel_table(scale_ids, reaches, offsets):
    taps = (2 * offsets + 1) * BLK
    lag = jnp.arange(taps, dtype=jnp.int32) - offsets * BLK
    within = jnp.arange(BLK, dtype=jnp.int32)
    scale_width = 2.0 * TD * jnp.exp2((scale_ids - (NS - 1)).astype(jnp.float32) / 4.0)
    width = scale_width[:, None, None]
    offset = lag[None, :, None] - within[None, None, :]
    scaled_offset = offset.astype(jnp.float32) / width
    amplitude = math.pi ** (-0.25) * lax.rsqrt(width) * jnp.exp(-0.5 * scaled_offset * scaled_offset)
    inside = jnp.abs(offset) < (reaches * BLK)[:, None, None]
    lag_phase = 6.0 * (lag.astype(jnp.float32)[None, :] / scale_width[:, None])
    time_phase = 6.0 * (within.astype(jnp.float32)[None, :] / scale_width[:, None])
    lag_cos = jnp.cos(lag_phase)[:, :, None]
    lag_sin = jnp.sin(lag_phase)[:, :, None]
    time_cos = jnp.cos(time_phase)[:, None, :]
    time_sin = jnp.sin(time_phase)[:, None, :]
    cos_part = lag_cos * time_cos + lag_sin * time_sin
    sin_part = lag_sin * time_cos - lag_cos * time_sin
    real_part = jnp.where(inside, amplitude * cos_part, 0.0).astype(jnp.bfloat16)
    imag_part = jnp.where(inside, amplitude * sin_part, 0.0).astype(jnp.bfloat16)
    return jnp.stack([real_part, imag_part], axis=1)


def band_coefficients(extended, scale_ids, reaches, offsets):
    channels = extended.shape[0]
    table = kernel_table(scale_ids, reaches, offsets)
    coefficients = jnp.einsum("cm,qrmt->qrct", extended, table, preferred_element_type=jnp.float32)
    scale_count = scale_ids.shape[0]
    return coefficients.astype(jnp.bfloat16).reshape(scale_count, 2 * channels, BLK)


def pair_sums(coefficients, first_flat, second_flat):
    scale_count = coefficients.shape[0]
    channels = coefficients.shape[1] // 2
    time_span = coefficients.shape[2]
    chan_iota = jnp.arange(channels, dtype=jnp.int32)
    both = jnp.concatenate([first_flat, second_flat])
    pick = (both[:, None] == chan_iota[None, :]).astype(jnp.bfloat16)
    parts = coefficients.reshape(scale_count, 2, channels, time_span)
    picked = jnp.einsum("pc,qrct->qrpt", pick, parts, preferred_element_type=jnp.bfloat16)
    pairs = first_flat.shape[0]
    first_real = picked[:, 0, :pairs]
    first_imag = picked[:, 1, :pairs]
    second_real = picked[:, 0, pairs:]
    second_imag = picked[:, 1, pairs:]

    def time_sum(left, right):
        return jnp.einsum("qpt,qpt->qp", left, right, preferred_element_type=jnp.float32)

    cross_real = time_sum(first_real, second_real) + time_sum(first_imag, second_imag)
    cross_imag = time_sum(first_imag, second_real) - time_sum(first_real, second_imag)
    power = jnp.einsum("qrct,qrct->qc", parts, parts, preferred_element_type=jnp.float32)
    high = lax.reduce_precision(power, exponent_bits=8, mantissa_bits=7)
    rest = power - high
    middle = lax.reduce_precision(rest, exponent_bits=8, mantissa_bits=7)
    low = rest - middle
    pieces = jnp.stack([high, middle, low]).astype(jnp.bfloat16)
    picked_power = jnp.einsum("pc,kqc->kqp", pick, pieces, preferred_element_type=jnp.float32)
    owner_power = (picked_power[0] + picked_power[1]) + picked_power[2]
    power_first = owner_power[:, :pairs]
    power_second = owner_power[:, pairs:]
    return jnp.stack([cross_real, cross_imag, power_first, power_second], axis=1)


def shards(signal, support, pair_first, pair_second, pair_count):
    groups = lax.axis_size("chan")
    cluster_number = lax.axis_index("chan")
    time_index = lax.axis_index("tm")
    time_devices = lax.axis_size("tm")
    time_span = signal.shape[1]
    ntime = time_span * time_devices
    rounded = signal.astype(jnp.bfloat16)
    gathered = lax.all_gather(rounded, "chan", axis=0, tiled=True)
    near = jnp.concatenate(
        [from_behind(gathered, "tm", 1), gathered, from_behind(gathered, "tm", -1)], axis=1
    )
    wide = jnp.concatenate([from_behind(near, "tm", 3), near, from_behind(near, "tm", -3)], axis=1)
    per_group = NS // groups
    band = NS // 4
    narrow_count = (NS - band) // groups
    wide_count = band // groups
    narrow_ids = cluster_number * narrow_count + jnp.arange(narrow_count, dtype=jnp.int32)
    wide_ids = NS - band + cluster_number * wide_count + jnp.arange(wide_count, dtype=jnp.int32)
    narrow_coefficients = band_coefficients(near, narrow_ids, support[narrow_ids], 1)
    wide_coefficients = band_coefficients(wide, wide_ids, support[wide_ids], 4)
    owner_devices, slots_total = pair_first.shape
    slots_local = slots_total // time_devices

    def by_block(pairs):
        return pairs.reshape(owner_devices, time_devices, slots_local).transpose(1, 0, 2).reshape(-1)

    first_flat = by_block(pair_first)
    second_flat = by_block(pair_second)
    sums = jnp.concatenate(
        [
            pair_sums(narrow_coefficients, first_flat, second_flat),
            pair_sums(wide_coefficients, first_flat, second_flat),
        ],
        axis=0,
    )
    values = sums.shape[1]
    destinations = time_devices * groups
    partial_value = sums.reshape(per_group * values, -1).T.reshape(destinations, -1)
    exchanged = lax.all_to_all(partial_value, ("tm", "chan"), 0, 0, tiled=True)
    summed = jnp.sum(exchanged.reshape(time_devices, groups, -1), axis=0)
    owned = summed.reshape(groups, slots_local, per_group, values).transpose(1, 3, 0, 2) / ntime
    owned = jnp.concatenate(
        [
            owned[:, :, :, :narrow_count].reshape(slots_local, values, groups * narrow_count),
            owned[:, :, :, narrow_count:].reshape(slots_local, values, groups * wide_count),
        ],
        axis=2,
    )
    slot_index = time_index * slots_local + jnp.arange(slots_local, dtype=jnp.int32)
    alive_mask = slot_index < pair_count[cluster_number]
    cross_real = owned[:, 0, :]
    cross_imag = owned[:, 1, :]
    first_power = owned[:, 2, :]
    second_power = owned[:, 3, :]
    coherence = (cross_real * cross_real + cross_imag * cross_imag) / (
        (first_power + power_floor) * (second_power + power_floor)
    )
    coherence = jnp.where(alive_mask[:, None], coherence, 0.0)[None]
    cross = jnp.where(alive_mask[:, None, None], owned[:, :2, :], 0.0)[None]
    return (cross, coherence.astype(jnp.float32))


def solution(mesh):
    in_specs = (P("chan", "tm"), P(), P(), P(), P())
    out_specs = (P("chan", "tm", None, None), P("chan", "tm", None))
    return jax.shard_map(shards, mesh=mesh, in_specs=in_specs, out_specs=out_specs, check_vma=False)
```

```python
import math

import jax
import jax.numpy as jnp
import numpy as np
from jax import lax
from jax.sharding import PartitionSpec as P

NS = 32
BLK = 128
TD = 128


power_floor = 1e-06


def from_behind(array, axis, by):
    peers = lax.axis_size(axis)
    return lax.ppermute(array, axis, [(i, (i + by) % peers) for i in range(peers)])


def kernel_table(scale_ids, reaches, offsets):
    taps = (2 * offsets + 1) * BLK
    lag = jnp.arange(taps, dtype=jnp.int32) - offsets * BLK
    within = jnp.arange(BLK, dtype=jnp.int32)
    scale_width = 2.0 * TD * jnp.exp2((scale_ids - (NS - 1)).astype(jnp.float32) / 4.0)
    width = scale_width[:, None, None]
    offset = lag[None, :, None] - within[None, None, :]
    scaled_offset = offset.astype(jnp.float32) / width
    amplitude = math.pi ** (-0.25) * lax.rsqrt(width) * jnp.exp(-0.5 * scaled_offset * scaled_offset)
    inside = jnp.abs(offset) < (reaches * BLK)[:, None, None]
    lag_phase = 6.0 * (lag.astype(jnp.float32)[None, :] / scale_width[:, None])
    time_phase = 6.0 * (within.astype(jnp.float32)[None, :] / scale_width[:, None])
    lag_cos = jnp.cos(lag_phase)[:, :, None]
    lag_sin = jnp.sin(lag_phase)[:, :, None]
    time_cos = jnp.cos(time_phase)[:, None, :]
    time_sin = jnp.sin(time_phase)[:, None, :]
    cos_part = lag_cos * time_cos + lag_sin * time_sin
    sin_part = lag_sin * time_cos - lag_cos * time_sin
    real_part = jnp.where(inside, amplitude * cos_part, 0.0).astype(jnp.bfloat16)
    imag_part = jnp.where(inside, amplitude * sin_part, 0.0).astype(jnp.bfloat16)
    return jnp.stack([real_part, imag_part], axis=1)


def band_coefficients(extended, scale_ids, reaches, offsets):
    channels = extended.shape[0]
    table = kernel_table(scale_ids, reaches, offsets)
    coefficients = jnp.einsum("cm,qrmt->qrct", extended, table, preferred_element_type=jnp.float32)
    scale_count = scale_ids.shape[0]
    return coefficients.astype(jnp.bfloat16).reshape(scale_count, 2 * channels, BLK)


def pair_sums(coefficients, first_flat, second_flat):
    scale_count = coefficients.shape[0]
    channels = coefficients.shape[1] // 2
    time_span = coefficients.shape[2]
    chan_iota = jnp.arange(channels, dtype=jnp.int32)
    both = jnp.concatenate([first_flat, second_flat])
    pick = (both[:, None] == chan_iota[None, :]).astype(jnp.bfloat16)
    parts = coefficients.reshape(scale_count, 2, channels, time_span)
    picked = jnp.einsum("pc,qrct->qrpt", pick, parts, preferred_element_type=jnp.bfloat16)
    pairs = first_flat.shape[0]
    first_real = picked[:, 0, :pairs]
    first_imag = picked[:, 1, :pairs]
    second_real = picked[:, 0, pairs:]
    second_imag = picked[:, 1, pairs:]

    def time_sum(left, right):
        return jnp.einsum("qpt,qpt->qp", left, right, preferred_element_type=jnp.float32)

    cross_real = time_sum(first_real, second_real) + time_sum(first_imag, second_imag)
    cross_imag = time_sum(first_imag, second_real) - time_sum(first_real, second_imag)
    power = jnp.einsum("qrct,qrct->qc", parts, parts, preferred_element_type=jnp.float32)
    high = lax.reduce_precision(power, exponent_bits=8, mantissa_bits=7)
    rest = power - high
    middle = lax.reduce_precision(rest, exponent_bits=8, mantissa_bits=7)
    low = rest - middle
    pieces = jnp.stack([high, middle, low]).astype(jnp.bfloat16)
    picked_power = jnp.einsum("pc,kqc->kqp", pick, pieces, preferred_element_type=jnp.float32)
    owner_power = (picked_power[0] + picked_power[1]) + picked_power[2]
    power_first = owner_power[:, :pairs]
    power_second = owner_power[:, pairs:]
    return jnp.stack([cross_real, cross_imag, power_first, power_second], axis=1)


def shards(signal, support, pair_first, pair_second, pair_count):
    groups = lax.axis_size("chan")
    cluster_number = lax.axis_index("chan")
    time_index = lax.axis_index("tm")
    time_devices = lax.axis_size("tm")
    time_span = signal.shape[1]
    ntime = time_span * time_devices
    rounded = signal.astype(jnp.bfloat16)
    sides = jnp.concatenate(
        [from_behind(rounded, "tm", 1), from_behind(rounded, "tm", -1)], axis=1
    )
    gathered = lax.all_gather(rounded, "chan", axis=0, tiled=True)
    sides = lax.all_gather(sides, "chan", axis=0, tiled=True)
    span = rounded.shape[1]
    near = jnp.concatenate([sides[:, :span], gathered, sides[:, span:]], axis=1)
    wide = jnp.concatenate([from_behind(near, "tm", 3), near, from_behind(near, "tm", -3)], axis=1)
    per_group = NS // groups
    band = NS // 4
    narrow_count = (NS - band) // groups
    wide_count = band // groups
    narrow_ids = cluster_number * narrow_count + jnp.arange(narrow_count, dtype=jnp.int32)
    wide_ids = NS - band + cluster_number * wide_count + jnp.arange(wide_count, dtype=jnp.int32)
    narrow_coefficients = band_coefficients(near, narrow_ids, support[narrow_ids], 1)
    wide_coefficients = band_coefficients(wide, wide_ids, support[wide_ids], 4)
    owner_devices, slots_total = pair_first.shape
    slots_local = slots_total // time_devices

    def by_block(pairs):
        return pairs.reshape(owner_devices, time_devices, slots_local).transpose(1, 0, 2).reshape(-1)

    first_flat = by_block(pair_first)
    second_flat = by_block(pair_second)
    sums = jnp.concatenate(
        [
            pair_sums(narrow_coefficients, first_flat, second_flat),
            pair_sums(wide_coefficients, first_flat, second_flat),
        ],
        axis=0,
    )
    values = sums.shape[1]
    destinations = time_devices * groups
    partial_value = sums.reshape(per_group * values, -1).T.reshape(destinations, -1)
    exchanged = lax.all_to_all(partial_value, ("tm", "chan"), 0, 0, tiled=True)
    summed = jnp.sum(exchanged.reshape(time_devices, groups, -1), axis=0)
    owned = summed.reshape(groups, slots_local, per_group, values).transpose(0, 2, 3, 1) / ntime
    owned = owned.reshape(groups, per_group, values, slots_local)
    owned = jnp.concatenate(
        [
            owned[:, :narrow_count].reshape(groups * narrow_count, values, slots_local),
            owned[:, narrow_count:].reshape(groups * wide_count, values, slots_local),
        ],
        axis=0,
    )
    slot_index = time_index * slots_local + jnp.arange(slots_local, dtype=jnp.int32)
    alive_mask = slot_index < pair_count[cluster_number]
    cross_real = owned[:, 0, :].T
    cross_imag = owned[:, 1, :].T
    first_power = owned[:, 2, :].T
    second_power = owned[:, 3, :].T
    coherence = (cross_real * cross_real + cross_imag * cross_imag) / (
        (first_power + power_floor) * (second_power + power_floor)
    )
    coherence = jnp.where(alive_mask[:, None], coherence, 0.0)[None]
    cross = jnp.stack([cross_real, cross_imag], axis=1)
    cross = jnp.where(alive_mask[:, None, None], cross, 0.0)[None]
    return (cross, coherence.astype(jnp.float32))


def solution(mesh):
    in_specs = (P("chan", "tm"), P(), P(), P(), P())
    out_specs = (P("chan", "tm", None, None), P("chan", "tm", None))
    return jax.shard_map(shards, mesh=mesh, in_specs=in_specs, out_specs=out_specs, check_vma=False)
```

```python
import math

import jax
import jax.numpy as jnp
import numpy as np
from jax import lax
from jax.sharding import PartitionSpec as P

NS = 32
BLK = 128
TD = 128


power_floor = 1e-06


def from_behind(array, axis, by):
    peers = lax.axis_size(axis)
    return lax.ppermute(array, axis, [(i, (i + by) % peers) for i in range(peers)])


def kernel_table(scale_ids, reaches, offsets):
    taps = (2 * offsets + 1) * BLK
    lag = jnp.arange(taps, dtype=jnp.int32) - offsets * BLK
    within = jnp.arange(BLK, dtype=jnp.int32)
    scale_width = 2.0 * TD * jnp.exp2((scale_ids - (NS - 1)).astype(jnp.float32) / 4.0)
    width = scale_width[:, None, None]
    offset = lag[None, :, None] - within[None, None, :]
    scaled_offset = offset.astype(jnp.float32) / width
    amplitude = math.pi ** (-0.25) * lax.rsqrt(width) * jnp.exp(-0.5 * scaled_offset * scaled_offset)
    inside = jnp.abs(offset) < (reaches * BLK)[:, None, None]
    lag_phase = 6.0 * (lag.astype(jnp.float32)[None, :] / scale_width[:, None])
    time_phase = 6.0 * (within.astype(jnp.float32)[None, :] / scale_width[:, None])
    lag_cos = jnp.cos(lag_phase)[:, :, None]
    lag_sin = jnp.sin(lag_phase)[:, :, None]
    time_cos = jnp.cos(time_phase)[:, None, :]
    time_sin = jnp.sin(time_phase)[:, None, :]
    cos_part = lag_cos * time_cos + lag_sin * time_sin
    sin_part = lag_sin * time_cos - lag_cos * time_sin
    real_part = jnp.where(inside, amplitude * cos_part, 0.0).astype(jnp.bfloat16)
    imag_part = jnp.where(inside, amplitude * sin_part, 0.0).astype(jnp.bfloat16)
    return jnp.stack([real_part, imag_part], axis=1)


def band_coefficients(extended, scale_ids, reaches, offsets):
    channels = extended.shape[0]
    table = kernel_table(scale_ids, reaches, offsets)
    coefficients = jnp.einsum("cm,qrmt->qrct", extended, table, preferred_element_type=jnp.float32)
    scale_count = scale_ids.shape[0]
    return coefficients.astype(jnp.bfloat16).reshape(scale_count, 2 * channels, BLK)


def pair_sums(coefficients, first_flat, second_flat):
    scale_count = coefficients.shape[0]
    channels = coefficients.shape[1] // 2
    time_span = coefficients.shape[2]
    chan_iota = jnp.arange(channels, dtype=jnp.int32)
    both = jnp.concatenate([first_flat, second_flat])
    pick = (both[:, None] == chan_iota[None, :]).astype(jnp.bfloat16)
    parts = coefficients.reshape(scale_count, 2, channels, time_span)
    picked = jnp.einsum("pc,qrct->qrpt", pick, parts, preferred_element_type=jnp.bfloat16)
    pairs = first_flat.shape[0]
    first_real = picked[:, 0, :pairs]
    first_imag = picked[:, 1, :pairs]
    second_real = picked[:, 0, pairs:]
    second_imag = picked[:, 1, pairs:]

    def time_sum(left, right):
        return jnp.einsum("qpt,qpt->qp", left, right, preferred_element_type=jnp.float32)

    cross_real = time_sum(first_real, second_real) + time_sum(first_imag, second_imag)
    cross_imag = time_sum(first_imag, second_real) - time_sum(first_real, second_imag)
    power = jnp.einsum("qrct,qrct->qc", parts, parts, preferred_element_type=jnp.float32)
    high = lax.reduce_precision(power, exponent_bits=8, mantissa_bits=7)
    rest = power - high
    middle = lax.reduce_precision(rest, exponent_bits=8, mantissa_bits=7)
    low = rest - middle
    pieces = jnp.stack([high, middle, low]).astype(jnp.bfloat16)
    picked_power = jnp.einsum("pc,kqc->kqp", pick, pieces, preferred_element_type=jnp.float32)
    owner_power = (picked_power[0] + picked_power[1]) + picked_power[2]
    power_first = owner_power[:, :pairs]
    power_second = owner_power[:, pairs:]
    return jnp.stack([cross_real, cross_imag, power_first, power_second], axis=1)


def shards(signal, support, pair_first, pair_second, pair_count):
    groups = lax.axis_size("chan")
    cluster_number = lax.axis_index("chan")
    time_index = lax.axis_index("tm")
    time_devices = lax.axis_size("tm")
    time_span = signal.shape[1]
    ntime = time_span * time_devices
    rounded = signal.astype(jnp.bfloat16)
    gathered = lax.all_gather(rounded, "chan", axis=0, tiled=True)
    near = jnp.concatenate(
        [from_behind(gathered, "tm", 1), gathered, from_behind(gathered, "tm", -1)], axis=1
    )
    wide = jnp.concatenate([from_behind(near, "tm", 3), near, from_behind(near, "tm", -3)], axis=1)
    per_group = NS // groups
    band = NS // 4
    narrow_count = (NS - band) // groups
    wide_count = band // groups
    narrow_ids = cluster_number * narrow_count + jnp.arange(narrow_count, dtype=jnp.int32)
    wide_ids = NS - band + cluster_number * wide_count + jnp.arange(wide_count, dtype=jnp.int32)
    narrow_coefficients = band_coefficients(near, narrow_ids, support[narrow_ids], 1)
    wide_coefficients = band_coefficients(wide, wide_ids, support[wide_ids], 4)
    owner_devices, slots_total = pair_first.shape
    slots_local = slots_total // time_devices

    def by_block(pairs):
        return pairs.reshape(owner_devices, time_devices, slots_local).transpose(1, 0, 2).reshape(-1)

    first_flat = by_block(pair_first)
    second_flat = by_block(pair_second)
    sums = jnp.concatenate(
        [
            pair_sums(narrow_coefficients, first_flat, second_flat),
            pair_sums(wide_coefficients, first_flat, second_flat),
        ],
        axis=0,
    )
    values = sums.shape[1]
    destinations = time_devices * groups
    partial_value = sums.reshape(per_group * values, -1).T.reshape(destinations, 2, -1)
    exchanged = lax.all_to_all(partial_value, ("tm", "chan"), 0, 0, tiled=True)
    summed = jnp.sum(exchanged.reshape(time_devices, groups, -1), axis=0)
    owned = summed.reshape(groups, slots_local, per_group, values).transpose(0, 2, 3, 1) / ntime
    owned = owned.reshape(groups, per_group, values, slots_local)
    owned = jnp.concatenate(
        [
            owned[:, :narrow_count].reshape(groups * narrow_count, values, slots_local),
            owned[:, narrow_count:].reshape(groups * wide_count, values, slots_local),
        ],
        axis=0,
    )
    slot_index = time_index * slots_local + jnp.arange(slots_local, dtype=jnp.int32)
    alive_mask = slot_index < pair_count[cluster_number]
    cross_real = owned[:, 0, :].T
    cross_imag = owned[:, 1, :].T
    first_power = owned[:, 2, :].T
    second_power = owned[:, 3, :].T
    coherence = (cross_real * cross_real + cross_imag * cross_imag) / (
        (first_power + power_floor) * (second_power + power_floor)
    )
    coherence = jnp.where(alive_mask[:, None], coherence, 0.0)[None]
    cross = jnp.stack([cross_real, cross_imag], axis=1)
    cross = jnp.where(alive_mask[:, None, None], cross, 0.0)[None]
    return (cross, coherence.astype(jnp.float32))


def solution(mesh):
    in_specs = (P("chan", "tm"), P(), P(), P(), P())
    out_specs = (P("chan", "tm", None, None), P("chan", "tm", None))
    return jax.shard_map(shards, mesh=mesh, in_specs=in_specs, out_specs=out_specs, check_vma=False)
```

```python
import math

import jax
import jax.numpy as jnp
import numpy as np
from jax import lax
from jax.sharding import PartitionSpec as P

NS = 32
BLK = 128
TD = 128


power_floor = 1e-06


def from_behind(array, axis, by):
    peers = lax.axis_size(axis)
    return lax.ppermute(array, axis, [(i, (i + by) % peers) for i in range(peers)])


def kernel_table(scale_ids, reaches, offsets):
    taps = (2 * offsets + 1) * BLK
    lag = jnp.arange(taps, dtype=jnp.int32) - offsets * BLK
    within = jnp.arange(BLK, dtype=jnp.int32)
    scale_width = 2.0 * TD * jnp.exp2((scale_ids - (NS - 1)).astype(jnp.float32) / 4.0)
    width = scale_width[:, None, None]
    offset = lag[None, :, None] - within[None, None, :]
    scaled_offset = offset.astype(jnp.float32) / width
    amplitude = math.pi ** (-0.25) * lax.rsqrt(width) * jnp.exp(-0.5 * scaled_offset * scaled_offset)
    inside = jnp.abs(offset) < (reaches * BLK)[:, None, None]
    lag_phase = 6.0 * (lag.astype(jnp.float32)[None, :] / scale_width[:, None])
    time_phase = 6.0 * (within.astype(jnp.float32)[None, :] / scale_width[:, None])
    lag_cos = jnp.cos(lag_phase)[:, :, None]
    lag_sin = jnp.sin(lag_phase)[:, :, None]
    time_cos = jnp.cos(time_phase)[:, None, :]
    time_sin = jnp.sin(time_phase)[:, None, :]
    cos_part = lag_cos * time_cos + lag_sin * time_sin
    sin_part = lag_sin * time_cos - lag_cos * time_sin
    real_part = jnp.where(inside, amplitude * cos_part, 0.0).astype(jnp.bfloat16)
    imag_part = jnp.where(inside, amplitude * sin_part, 0.0).astype(jnp.bfloat16)
    return jnp.stack([real_part, imag_part], axis=1)


def band_coefficients(extended, scale_ids, reaches, offsets):
    channels = extended.shape[0]
    table = kernel_table(scale_ids, reaches, offsets)
    coefficients = jnp.einsum("cm,qrmt->qrct", extended, table, preferred_element_type=jnp.float32)
    scale_count = scale_ids.shape[0]
    return coefficients.astype(jnp.bfloat16).reshape(scale_count, 2 * channels, BLK)


def pair_sums(coefficients, first_flat, second_flat):
    scale_count = coefficients.shape[0]
    channels = coefficients.shape[1] // 2
    time_span = coefficients.shape[2]
    chan_iota = jnp.arange(channels, dtype=jnp.int32)
    both = jnp.concatenate([first_flat, second_flat])
    pick = (both[:, None] == chan_iota[None, :]).astype(jnp.bfloat16)
    parts = coefficients.reshape(scale_count, 2, channels, time_span)
    picked = jnp.einsum("pc,qrct->qrpt", pick, parts, preferred_element_type=jnp.bfloat16)
    pairs = first_flat.shape[0]
    first_real = picked[:, 0, :pairs]
    first_imag = picked[:, 1, :pairs]
    second_real = picked[:, 0, pairs:]
    second_imag = picked[:, 1, pairs:]

    def time_sum(left, right):
        return jnp.einsum("qpt,qpt->qp", left, right, preferred_element_type=jnp.float32)

    cross_real = time_sum(first_real, second_real) + time_sum(first_imag, second_imag)
    cross_imag = time_sum(first_imag, second_real) - time_sum(first_real, second_imag)
    power = jnp.einsum("qrct,qrct->qc", parts, parts, preferred_element_type=jnp.float32)
    high = lax.reduce_precision(power, exponent_bits=8, mantissa_bits=7)
    rest = power - high
    middle = lax.reduce_precision(rest, exponent_bits=8, mantissa_bits=7)
    low = rest - middle
    pieces = jnp.stack([high, middle, low]).astype(jnp.bfloat16)
    picked_power = jnp.einsum("pc,kqc->kqp", pick, pieces, preferred_element_type=jnp.float32)
    owner_power = (picked_power[0] + picked_power[1]) + picked_power[2]
    power_first = owner_power[:, :pairs]
    power_second = owner_power[:, pairs:]
    return jnp.stack([cross_real, cross_imag, power_first, power_second], axis=1)


def shards(signal, support, pair_first, pair_second, pair_count):
    groups = lax.axis_size("chan")
    cluster_number = lax.axis_index("chan")
    time_index = lax.axis_index("tm")
    time_devices = lax.axis_size("tm")
    time_span = signal.shape[1]
    ntime = time_span * time_devices
    rounded = signal.astype(jnp.bfloat16)
    gathered = lax.all_gather(rounded, "chan", axis=0, tiled=True)
    near = jnp.concatenate(
        [from_behind(gathered, "tm", 1), gathered, from_behind(gathered, "tm", -1)], axis=1
    )
    wide = jnp.concatenate([from_behind(near, "tm", 3), near, from_behind(near, "tm", -3)], axis=1)
    per_group = NS // groups
    band = NS // 4
    narrow_count = (NS - band) // groups
    wide_count = band // groups
    narrow_ids = cluster_number * narrow_count + jnp.arange(narrow_count, dtype=jnp.int32)
    wide_ids = NS - band + cluster_number * wide_count + jnp.arange(wide_count, dtype=jnp.int32)
    narrow_coefficients = band_coefficients(near, narrow_ids, support[narrow_ids], 1)
    wide_coefficients = band_coefficients(wide, wide_ids, support[wide_ids], 4)
    owner_devices, slots_total = pair_first.shape
    slots_local = slots_total // time_devices

    def by_block(pairs):
        return pairs.reshape(owner_devices, time_devices, slots_local).transpose(2, 1, 0).reshape(-1)

    first_flat = by_block(pair_first)
    second_flat = by_block(pair_second)
    sums = jnp.concatenate(
        [
            pair_sums(narrow_coefficients, first_flat, second_flat),
            pair_sums(wide_coefficients, first_flat, second_flat),
        ],
        axis=0,
    )
    values = sums.shape[1]
    destinations = time_devices * groups
    partial_value = sums.reshape(per_group * values * slots_local, destinations).T
    partial_value = partial_value.reshape(destinations, 2, -1)
    exchanged = lax.all_to_all(partial_value, ("tm", "chan"), 0, 0, tiled=True)
    summed = jnp.sum(exchanged.reshape(time_devices, groups, -1), axis=0)
    owned = summed.reshape(groups, per_group, values, slots_local) / ntime
    owned = owned.reshape(groups, per_group, values, slots_local)
    owned = jnp.concatenate(
        [
            owned[:, :narrow_count].reshape(groups * narrow_count, values, slots_local),
            owned[:, narrow_count:].reshape(groups * wide_count, values, slots_local),
        ],
        axis=0,
    )
    slot_index = time_index * slots_local + jnp.arange(slots_local, dtype=jnp.int32)
    alive_mask = slot_index < pair_count[cluster_number]
    cross_real = owned[:, 0, :].T
    cross_imag = owned[:, 1, :].T
    first_power = owned[:, 2, :].T
    second_power = owned[:, 3, :].T
    coherence = (cross_real * cross_real + cross_imag * cross_imag) / (
        (first_power + power_floor) * (second_power + power_floor)
    )
    coherence = jnp.where(alive_mask[:, None], coherence, 0.0)[None]
    cross = jnp.stack([cross_real, cross_imag], axis=1)
    cross = jnp.where(alive_mask[:, None, None], cross, 0.0)[None]
    return (cross, coherence.astype(jnp.float32))


def solution(mesh):
    in_specs = (P("chan", "tm"), P(), P(), P(), P())
    out_specs = (P("chan", "tm", None, None), P("chan", "tm", None))
    return jax.shard_map(shards, mesh=mesh, in_specs=in_specs, out_specs=out_specs, check_vma=False)
```

```python
import math

import jax
import jax.numpy as jnp
import numpy as np
from jax import lax
from jax.sharding import PartitionSpec as P

NS = 32
BLK = 128
TD = 128


power_floor = 1e-06


def from_behind(array, axis, by):
    peers = lax.axis_size(axis)
    return lax.ppermute(array, axis, [(i, (i + by) % peers) for i in range(peers)])


def kernel_table(scale_ids, reaches, offsets):
    taps = (2 * offsets + 1) * BLK
    lag = jnp.arange(taps, dtype=jnp.int32) - offsets * BLK
    within = jnp.arange(BLK, dtype=jnp.int32)
    scale_width = 2.0 * TD * jnp.exp2((scale_ids - (NS - 1)).astype(jnp.float32) / 4.0)
    width = scale_width[:, None, None]
    offset = lag[None, :, None] - within[None, None, :]
    scaled_offset = offset.astype(jnp.float32) / width
    amplitude = math.pi ** (-0.25) * lax.rsqrt(width) * jnp.exp(-0.5 * scaled_offset * scaled_offset)
    inside = jnp.abs(offset) < (reaches * BLK)[:, None, None]
    lag_phase = 6.0 * (lag.astype(jnp.float32)[None, :] / scale_width[:, None])
    time_phase = 6.0 * (within.astype(jnp.float32)[None, :] / scale_width[:, None])
    lag_cos = jnp.cos(lag_phase)[:, :, None]
    lag_sin = jnp.sin(lag_phase)[:, :, None]
    time_cos = jnp.cos(time_phase)[:, None, :]
    time_sin = jnp.sin(time_phase)[:, None, :]
    cos_part = lag_cos * time_cos + lag_sin * time_sin
    sin_part = lag_sin * time_cos - lag_cos * time_sin
    real_part = jnp.where(inside, amplitude * cos_part, 0.0).astype(jnp.bfloat16)
    imag_part = jnp.where(inside, amplitude * sin_part, 0.0).astype(jnp.bfloat16)
    return jnp.stack([real_part, imag_part], axis=1)


def band_coefficients(extended, scale_ids, reaches, offsets):
    channels = extended.shape[0]
    table = kernel_table(scale_ids, reaches, offsets)
    coefficients = jnp.einsum("cm,qrmt->qrct", extended, table, preferred_element_type=jnp.float32)
    scale_count = scale_ids.shape[0]
    return coefficients.astype(jnp.bfloat16).reshape(scale_count, 2 * channels, BLK)


def pair_sums(coefficients, first_flat, second_flat):
    scale_count = coefficients.shape[0]
    channels = coefficients.shape[1] // 2
    time_span = coefficients.shape[2]
    chan_iota = jnp.arange(channels, dtype=jnp.int32)
    both = jnp.concatenate([first_flat, second_flat])
    pick = (both[:, None] == chan_iota[None, :]).astype(jnp.bfloat16)
    parts = coefficients.reshape(scale_count, 2, channels, time_span)
    picked = jnp.einsum("pc,qrct->qrpt", pick, parts, preferred_element_type=jnp.bfloat16)
    pairs = first_flat.shape[0]
    first_real = picked[:, 0, :pairs]
    first_imag = picked[:, 1, :pairs]
    second_real = picked[:, 0, pairs:]
    second_imag = picked[:, 1, pairs:]

    def time_sum(left, right):
        return jnp.einsum("qpt,qpt->qp", left, right, preferred_element_type=jnp.float32)

    cross_real = time_sum(first_real, second_real) + time_sum(first_imag, second_imag)
    cross_imag = time_sum(first_imag, second_real) - time_sum(first_real, second_imag)
    power = jnp.einsum("qrct,qrct->qc", parts, parts, preferred_element_type=jnp.float32)
    high = lax.reduce_precision(power, exponent_bits=8, mantissa_bits=7)
    rest = power - high
    middle = lax.reduce_precision(rest, exponent_bits=8, mantissa_bits=7)
    low = rest - middle
    pieces = jnp.stack([high, middle, low]).astype(jnp.bfloat16)
    picked_power = jnp.einsum("pc,kqc->kqp", pick, pieces, preferred_element_type=jnp.float32)
    owner_power = (picked_power[0] + picked_power[1]) + picked_power[2]
    power_first = owner_power[:, :pairs]
    power_second = owner_power[:, pairs:]
    return jnp.stack([cross_real, cross_imag, power_first, power_second], axis=1)


def shards(signal, support, pair_first, pair_second, pair_count):
    groups = lax.axis_size("chan")
    cluster_number = lax.axis_index("chan")
    time_index = lax.axis_index("tm")
    time_devices = lax.axis_size("tm")
    time_span = signal.shape[1]
    ntime = time_span * time_devices
    rounded = signal.astype(jnp.bfloat16)
    gathered = lax.all_gather(rounded, "chan", axis=0, tiled=True)
    near = jnp.concatenate(
        [from_behind(gathered, "tm", 1), gathered, from_behind(gathered, "tm", -1)], axis=1
    )
    wide = jnp.concatenate([from_behind(near, "tm", 3), near, from_behind(near, "tm", -3)], axis=1)
    per_group = NS // groups
    band = NS // 4
    narrow_count = (NS - band) // groups
    wide_count = band // groups
    narrow_ids = cluster_number * narrow_count + jnp.arange(narrow_count, dtype=jnp.int32)
    wide_ids = NS - band + cluster_number * wide_count + jnp.arange(wide_count, dtype=jnp.int32)
    narrow_coefficients = band_coefficients(near, narrow_ids, support[narrow_ids], 1)
    wide_coefficients = band_coefficients(wide, wide_ids, support[wide_ids], 4)
    owner_devices, slots_total = pair_first.shape
    slots_local = slots_total // time_devices

    def by_block(pairs):
        return pairs.reshape(owner_devices, time_devices, slots_local).transpose(1, 0, 2).reshape(-1)

    first_flat = by_block(pair_first)
    second_flat = by_block(pair_second)
    sums = jnp.concatenate(
        [
            pair_sums(narrow_coefficients, first_flat, second_flat),
            pair_sums(wide_coefficients, first_flat, second_flat),
        ],
        axis=0,
    )
    values = sums.shape[1]
    destinations = time_devices * groups
    partial_value = sums.reshape(per_group * values, -1).T.reshape(destinations, 2, -1)
    exchanged = lax.all_to_all(partial_value, ("tm", "chan"), 0, 0, tiled=True)
    summed = jnp.sum(exchanged.reshape(time_devices, groups, -1), axis=0)
    owned = summed.reshape(groups, slots_local, per_group, values).transpose(1, 3, 0, 2) / ntime
    owned = jnp.concatenate(
        [
            owned[:, :, :, :narrow_count].reshape(slots_local, values, groups * narrow_count),
            owned[:, :, :, narrow_count:].reshape(slots_local, values, groups * wide_count),
        ],
        axis=2,
    )
    slot_index = time_index * slots_local + jnp.arange(slots_local, dtype=jnp.int32)
    alive_mask = slot_index < pair_count[cluster_number]
    cross_real = owned[:, 0, :]
    cross_imag = owned[:, 1, :]
    first_power = owned[:, 2, :]
    second_power = owned[:, 3, :]
    coherence = (cross_real * cross_real + cross_imag * cross_imag) / (
        (first_power + power_floor) * (second_power + power_floor)
    )
    coherence = jnp.where(alive_mask[:, None], coherence, 0.0)[None]
    cross = jnp.where(alive_mask[:, None, None], owned[:, :2, :], 0.0)[None]
    return (cross, coherence.astype(jnp.float32))


def solution(mesh):
    in_specs = (P("chan", "tm"), P(), P(), P(), P())
    out_specs = (P("chan", "tm", None, None), P("chan", "tm", None))
    return jax.shard_map(shards, mesh=mesh, in_specs=in_specs, out_specs=out_specs, check_vma=False)
```
